32 devices in a mesh: tm: 8 (over z, x), space: 4 (over y, core).
Axes of the slice: x: 2, y: 2, z: 4, core: 2. Of those that a mesh axis runs over, the one named last changes fastest.
Arguments:
- video: bfloat16 [128, 4, 32, 128], P('tm', 'space'), may hold values from -6 to 6
- stem_weight: float32 [9, 16], replicated, may hold values from -2 to 2
- stem_bias: float32 [16], replicated, may hold values from -3 to 3
- spatial_weight: bfloat16 [2, 9, 16, 16], replicated, may hold values from -0.5 to 0.5
- temporal_weight: bfloat16 [2, 3, 16, 16], replicated, may hold values from -0.875 to 0.875
- temporal_bias: float32 [2, 16], replicated, may hold values from -3 to 3
- head_weight: float32 [16], replicated, may hold values from -1.5 to 1.5
- head_bias: float32 [1], replicated, may hold values from -3 to 3
Outputs:
- response: float32 [128, 4, 32, 128], P('tm', 'space')
The draws below stay inside these ranges and needn't reach their ends.
All inputs are finite; a program needn't handle non-finite values.
Results may differ from the reference program's by a relative error of at most 0.013.
Values may be sent and summed in bfloat16 or wider, within the bound.
No kernel may reach another device: no remote copies, remote signals or barrier semaphores. Data moves between devices by JAX's collectives and lax.ppermute only.
A program may use at most 256 MiB of HBM per device.

```python
import jax
import jax.numpy as jnp
from jax import lax

C = 16
TILE_H = 32
TILE_W = 128
F_DEV = 16
FRAMES = 128
TILES = 4
N_SPACE = 4


def block_scale(rng, shape, pieces, smallest, high):
    level, own = 1.0, jax.random.fold_in(rng, 6)
    for axis_at, blocks in pieces:
        steps = jnp.exp(jax.random.uniform(jax.random.fold_in(own, axis_at), (blocks,), jnp.float32, smallest / len(pieces), high / len(pieces)))
        level = level * jnp.repeat(steps, shape[axis_at] // blocks).reshape([-1 if axis == axis_at else 1 for axis in range(len(shape))])
    return level


def noise(rng, dims, scale, limit, split=(), kind=jnp.bfloat16):
    drawn = scale * jax.random.normal(rng, dims, jnp.float32)
    if split:
        drawn = drawn * block_scale(rng, dims, split, -0.22, 0.18)
    return jnp.clip(drawn, -limit, limit).astype(kind)


def setup_inputs(seed: int = 0) -> dict:
    key_list = jax.random.split(jax.random.key(seed), 9)
    return {
        "video": noise(key_list[0], (FRAMES, TILES, TILE_H, TILE_W), 1.0, 6.0, ((0, 8), (1, 4))),
        "stem_weight": noise(key_list[1], (9, C), 9 ** -0.5, 2.0, (), jnp.float32),
        "stem_bias": noise(key_list[2], (C,), 0.5, 3.0, (), jnp.float32),
        "spatial_weight": noise(key_list[3], (2, 9, C, C), (9 * C) ** -0.5, 0.5),
        "temporal_weight": noise(key_list[4], (2, 3, C, C), (3 * C) ** -0.5, 0.875),
        "temporal_bias": noise(key_list[5], (2, C), 0.5, 3.0, (), jnp.float32),
        "head_weight": noise(key_list[6], (C,), C ** -0.5, 1.5, (), jnp.float32),
        "head_bias": noise(key_list[7], (1,), 1.0, 3.0, (), jnp.float32),
    }


def stem_conv(padded, stem_weight, stem_bias):
    height = padded.shape[1] - 2
    width = padded.shape[2] - 2
    total = jnp.zeros((stem_weight.shape[1], padded.shape[0], height, width), jnp.float32)
    for dy in range(3):
        for dx in range(3):
            window = padded[:, dy:dy + height, dx:dx + width].astype(jnp.float32)
            total = total + stem_weight[3 * dy + dx][:, None, None, None] * window[None]
    return jax.nn.relu(total + stem_bias[:, None, None, None]).astype(jnp.bfloat16)


def spatial_conv(hidden, weight):
    padded = jnp.pad(hidden, ((0, 0), (0, 0), (1, 1), (1, 1)))
    height = hidden.shape[2]
    width = hidden.shape[3]
    total = jnp.zeros(hidden.shape, jnp.float32)
    for dy in range(3):
        for dx in range(3):
            window = padded[:, :, dy:dy + height, dx:dx + width].astype(jnp.float32)
            total = total + jnp.einsum('oc,cfhw->ofhw', weight[3 * dy + dx].astype(jnp.float32), window)
    return total


def temporal_conv(lead_s, weight, bias):
    count = lead_s.shape[1] - 2
    total = jnp.zeros((lead_s.shape[0], count, lead_s.shape[2], lead_s.shape[3]), jnp.float32)
    for j in range(3):
        total = total + jnp.einsum('oc,cfhw->ofhw', weight[j].astype(jnp.float32), lead_s[:, j:j + count].astype(jnp.float32))
    return total + bias[:, None, None, None]


def mask_frames(hidden, index, lead):
    count = hidden.shape[1]
    positions = index * F_DEV - lead + jnp.arange(count, dtype=jnp.int32)
    keep = positions >= 0
    return jnp.where(keep[None, :, None, None], hidden, jnp.zeros_like(hidden))


def reference(video, stem_weight, stem_bias, spatial_weight, temporal_weight, temporal_bias, head_weight, head_bias):
    grid_w = min(4, N_SPACE)
    grid_h = N_SPACE // grid_w
    frames = video.reshape(FRAMES, grid_h, grid_w, TILE_H, TILE_W).transpose(0, 1, 3, 2, 4)
    frames = frames.reshape(FRAMES, grid_h * TILE_H, grid_w * TILE_W)
    before = jnp.zeros((4, grid_h * TILE_H, grid_w * TILE_W), jnp.bfloat16)
    padded_video = jnp.concatenate([before, frames], axis=0)

    def one_block(index):
        start = (index * F_DEV).astype(jnp.int32)
        clip = lax.dynamic_slice_in_dim(padded_video, start, F_DEV + 4, 0)
        hidden = stem_conv(jnp.pad(clip, ((0, 0), (1, 1), (1, 1))), stem_weight, stem_bias)
        lead_count = 4
        hidden = mask_frames(hidden, index, lead_count)
        for block in range(2):
            s_now = spatial_conv(hidden, spatial_weight[block]).astype(jnp.bfloat16)
            t_now = temporal_conv(s_now, temporal_weight[block], temporal_bias[block])
            hidden = (hidden[:, 2:].astype(jnp.float32) + jax.nn.relu(t_now)).astype(jnp.bfloat16)
            lead_count = lead_count - 2
            hidden = mask_frames(hidden, index, lead_count)
        return jnp.sum(head_weight[:, None, None, None] * hidden.astype(jnp.float32), axis=0) + head_bias[0]

    outputs = lax.map(one_block, jnp.arange(FRAMES // F_DEV, dtype=jnp.int32))
    outputs = outputs.reshape(FRAMES, grid_h, TILE_H, grid_w, TILE_W).transpose(0, 1, 3, 2, 4)
    return outputs.reshape(FRAMES, grid_h * grid_w, TILE_H, TILE_W)
```

```python
import jax
import jax.numpy as jnp
from jax import lax
from jax.experimental import pallas as pl
from jax.experimental.pallas import tpu as pltpu
from jax.sharding import PartitionSpec as P

HALO = 3
LEAD = 4


def shifted(value, axis, steps):
    count = lax.axis_size(axis)
    leading, last = (max(0, -steps), min(count, count - steps))
    return lax.ppermute(value, axis, [(source, source + steps) for source in range(leading, last)])


def grid_shape():
    parts = lax.axis_size("space")
    grid_w = min(4, parts)
    return parts // grid_w, grid_w


def spread(field, width):
    grid_w = grid_shape()[1]
    column = lax.axis_index("space") % grid_w
    west_piece = field[..., -width:]
    east_piece = field[..., :width]
    west_piece = jnp.where(column < grid_w - 1, west_piece, jnp.zeros_like(west_piece))
    east_piece = jnp.where(column > 0, east_piece, jnp.zeros_like(east_piece))
    west = shifted(west_piece, "space", 1)
    east = shifted(east_piece, "space", -1)
    wide = jnp.concatenate([west, field, east], axis=-1)
    north = shifted(wide[..., -width:, :], "space", grid_w)
    south = shifted(wide[..., :width, :], "space", -grid_w)
    return jnp.concatenate([north, wide, south], axis=-2)


def round_up(value, step):
    return (value + step - 1) // step * step


def flat_masks(height, width, length):
    grid_h, grid_w = grid_shape()
    place = lax.axis_index("space")
    pitch = width + 2 * HALO
    q = jnp.arange(length)
    y = q // pitch - HALO
    x = q % pitch - HALO
    gy = place // grid_w * height + y
    gx = place % grid_w * width + x
    inside = (q < (height + 2 * HALO) * pitch) & (gy >= 0) & (gy < grid_h * height)
    inside = inside & (gx >= 0) & (gx < grid_w * width)
    rows = []
    for margin in (2, 1):
        keep = inside & (y >= -margin) & (y < height + margin) & (x >= -margin) & (x < width + margin)
        rows.append(keep.astype(jnp.float32))
    return jnp.stack(rows)[:, None, :]


def make_kernel(n_in, count, pitch, length, base, total):
    offs = [(dy - 1) * pitch + (dx - 1) for dy in range(3) for dx in range(3)]
    shifts = [(-(base + off)) % total for off in offs]

    def kernel(first_ref, vp_ref, mask_ref, wst_ref, bst_ref, wsp_ref, tw_ref, tb_ref, hw_ref, hb_ref,
               out_ref, ha_ref, hb2_ref, s_ref):
        first = first_ref[0]
        zeros_side = jnp.zeros((ha_ref.shape[1], base), jnp.bfloat16)

        def clear(ref, n):
            def body(f, carry):
                ref[f, :, 0:base] = zeros_side
                ref[f, :, base + length:total] = zeros_side
                return carry
            lax.fori_loop(0, n, body, 0)

        clear(ha_ref, n_in)
        clear(hb2_ref, n_in - 2)

        mask0 = mask_ref[0] > 0.5
        mask1 = mask_ref[1] > 0.5

        def stem(f, carry):
            acc = jnp.dot(wst_ref[...], vp_ref[f], preferred_element_type=jnp.float32)
            h0 = jnp.maximum(acc + bst_ref[...], 0.0).astype(jnp.bfloat16)
            keep = mask0 & (first + f >= 0)
            ha_ref[f, :, base:base + length] = jnp.where(keep, h0, jnp.zeros_like(h0))
            return carry

        lax.fori_loop(0, n_in, stem, 0)

        def spatial(block, src_ref, n):
            def body(f, carry):
                x = src_ref[f]
                pieces = [pltpu.roll(x, sh, 1)[:, :length] if sh else x[:, :length] for sh in shifts]
                patches = jnp.concatenate(pieces, axis=0)
                acc = jnp.dot(wsp_ref[block], patches, preferred_element_type=jnp.float32)
                s_ref[f] = acc.astype(jnp.bfloat16)
                return carry
            lax.fori_loop(0, n, body, 0)

        def temporal(block, src_ref, k):
            stacked = jnp.concatenate([s_ref[k], s_ref[k + 1], s_ref[k + 2]], axis=0)
            acc = jnp.dot(tw_ref[block], stacked, preferred_element_type=jnp.float32) + tb_ref[block]
            centre = src_ref[k + 2, :, base:base + length].astype(jnp.float32)
            return (centre + jnp.maximum(acc, 0.0)).astype(jnp.bfloat16)

        spatial(0, ha_ref, n_in)

        def block0(k, carry):
            h1 = temporal(0, ha_ref, k)
            keep = mask1 & (first + 2 + k >= 0)
            hb2_ref[k, :, base:base + length] = jnp.where(keep, h1, jnp.zeros_like(h1))
            return carry

        lax.fori_loop(0, n_in - 2, block0, 0)
        spatial(1, hb2_ref, n_in - 2)

        def block1(k, carry):
            h2 = temporal(1, hb2_ref, k).astype(jnp.float32)
            head = jnp.sum(hw_ref[...] * h2, axis=0, keepdims=True) + hb_ref[...]
            out_ref[k] = head
            return carry

        lax.fori_loop(0, count, block1, 0)

    return kernel


def shards(video, stem_weight, stem_bias, spatial_weight, temporal_weight, temporal_bias, head_weight, head_bias):
    clip = video[:, 0]
    count, height, width = clip.shape
    lead = shifted(clip[-LEAD:], "tm", 1)
    extended = spread(jnp.concatenate([lead, clip], axis=0), HALO)
    n_in = count + LEAD
    pitch = width + 2 * HALO
    rows = height + 2 * HALO
    length = round_up(rows * pitch, 128)
    base = round_up(pitch + 1, 128)
    total = length + 2 * base
    flat = extended.reshape(n_in, rows * pitch)
    flat = jnp.pad(flat, ((0, 0), (base, total - base - rows * pitch)))
    offs = [(dy - 1) * pitch + (dx - 1) for dy in range(3) for dx in range(3)]
    taps = jnp.stack([flat[:, base + off:base + off + length] for off in offs], axis=1)
    taps = jnp.pad(taps, ((0, 0), (0, 16 - len(offs)), (0, 0)))
    vp = jnp.concatenate([taps, taps], axis=1)

    channels = stem_weight.shape[1]
    w_hi = stem_weight.astype(jnp.bfloat16)
    w_lo = (stem_weight - w_hi.astype(jnp.float32)).astype(jnp.bfloat16)
    wst = jnp.zeros((channels, 32), jnp.bfloat16)
    wst = wst.at[:, 0:9].set(w_hi.T).at[:, 16:25].set(w_lo.T)
    bst = stem_bias.astype(jnp.float32)[:, None]
    wsp = spatial_weight.transpose(0, 2, 1, 3).reshape(2, channels, 9 * channels)
    tw = temporal_weight.transpose(0, 2, 1, 3).reshape(2, channels, 3 * channels)
    tb = temporal_bias.astype(jnp.float32)[:, :, None]
    hw = head_weight.astype(jnp.float32)[:, None]
    hb = head_bias.astype(jnp.float32).reshape(1, 1)
    masks = flat_masks(height, width, length)
    first = (lax.axis_index("tm") * count - LEAD).astype(jnp.int32).reshape(1)

    vmem = pltpu.MemorySpace.VMEM if hasattr(pltpu, "MemorySpace") else pltpu.TPUMemorySpace.VMEM
    smem = pltpu.MemorySpace.SMEM if hasattr(pltpu, "MemorySpace") else pltpu.TPUMemorySpace.SMEM
    spec = pl.BlockSpec(memory_space=vmem)
    out = pl.pallas_call(
        make_kernel(n_in, count, pitch, length, base, total),
        out_shape=jax.ShapeDtypeStruct((count, 1, length), jnp.float32),
        in_specs=[pl.BlockSpec(memory_space=smem)] + [spec] * 9,
        out_specs=spec,
        scratch_shapes=[
            pltpu.VMEM((n_in, channels, total), jnp.bfloat16),
            pltpu.VMEM((n_in - 2, channels, total), jnp.bfloat16),
            pltpu.VMEM((n_in, channels, length), jnp.bfloat16),
        ],
        compiler_params=pltpu.CompilerParams(vmem_limit_bytes=48 * 1024 * 1024),
    )(first, vp, masks, wst, bst, wsp, tw, tb, hw, hb)
    result = out[:, 0, : rows * pitch].reshape(count, rows, pitch)
    result = result[:, HALO:HALO + height, HALO:HALO + width]
    return result[:, None]


def solution(mesh):
    placed = (P("tm", "space", None, None), P(), P(), P(), P(), P(), P(), P())
    return jax.shard_map(
        shards, mesh=mesh, in_specs=placed, out_specs=P("tm", "space", None, None), check_vma=False
    )
```

```python
import jax
import jax.numpy as jnp
from jax import lax
from jax.experimental import pallas as pl
from jax.experimental.pallas import tpu as pltpu
from jax.sharding import PartitionSpec as P

HALO = 3
LEAD = 4


def shifted(value, axis, steps):
    count = lax.axis_size(axis)
    leading, last = (max(0, -steps), min(count, count - steps))
    if leading >= last:
        return jnp.zeros_like(value)
    return lax.ppermute(value, axis, [(source, source + steps) for source in range(leading, last)])


def grid_shape():
    parts = lax.axis_size("space")
    grid_w = min(4, parts)
    return parts // grid_w, grid_w


def spread(field, width):
    grid_w = grid_shape()[1]
    column = lax.axis_index("space") % grid_w
    west_piece = field[..., -width:]
    east_piece = field[..., :width]
    west_piece = jnp.where(column < grid_w - 1, west_piece, jnp.zeros_like(west_piece))
    east_piece = jnp.where(column > 0, east_piece, jnp.zeros_like(east_piece))
    west = shifted(west_piece, "space", 1)
    east = shifted(east_piece, "space", -1)
    wide = jnp.concatenate([west, field, east], axis=-1)
    north = shifted(wide[..., -width:, :], "space", grid_w)
    south = shifted(wide[..., :width, :], "space", -grid_w)
    return jnp.concatenate([north, wide, south], axis=-2)


def round_up(value, step):
    return (value + step - 1) // step * step


def flat_masks(height, width, length):
    grid_h, grid_w = grid_shape()
    place = lax.axis_index("space")
    pitch = width + 2 * HALO
    q = jnp.arange(length)
    y = q // pitch - HALO
    x = q % pitch - HALO
    gy = place // grid_w * height + y
    gx = place % grid_w * width + x
    inside = (q < (height + 2 * HALO) * pitch) & (gy >= 0) & (gy < grid_h * height)
    inside = inside & (gx >= 0) & (gx < grid_w * width)
    rows = []
    for margin in (2, 1):
        keep = inside & (y >= -margin) & (y < height + margin) & (x >= -margin) & (x < width + margin)
        rows.append(keep.astype(jnp.float32))
    return jnp.stack(rows)[:, None, :]


def make_kernel(n_in, count, pitch, length, base, total):
    offs = [(dy - 1) * pitch + (dx - 1) for dy in range(3) for dx in range(3)]
    shifts = [(-(base + off)) % total for off in offs]

    def kernel(first_ref, vp_ref, mask_ref, wst_ref, bst_ref, wsp_ref, tw_ref, tb_ref, hw_ref, hb_ref,
               out_ref, ha_ref, hb2_ref, s_ref):
        first = first_ref[0]
        zeros_side = jnp.zeros((ha_ref.shape[1], base), jnp.bfloat16)

        def clear(ref, n):
            def body(f, carry):
                ref[f, :, 0:base] = zeros_side
                ref[f, :, base + length:total] = zeros_side
                return carry
            lax.fori_loop(0, n, body, 0)

        clear(ha_ref, n_in)
        clear(hb2_ref, n_in - 2)

        mask0 = mask_ref[0] > 0.5
        mask1 = mask_ref[1] > 0.5

        filler = jnp.zeros((16 - len(shifts), length), jnp.float32)

        def stem(f, carry):
            v = vp_ref[f]
            rows = [pltpu.roll(v, sh, 1)[:, :length] if sh else v[:, :length] for sh in shifts]
            patch = jnp.concatenate(rows + [filler], axis=0).astype(jnp.bfloat16)
            patch = jnp.concatenate([patch, patch], axis=0)
            acc = jnp.dot(wst_ref[...], patch, preferred_element_type=jnp.float32)
            h0 = jnp.maximum(acc + bst_ref[...], 0.0).astype(jnp.bfloat16)
            keep = mask0 & (first + f >= 0)
            ha_ref[f, :, base:base + length] = jnp.where(keep, h0, jnp.zeros_like(h0))
            return carry

        lax.fori_loop(0, n_in, stem, 0)

        def spatial(block, src_ref, n):
            def body(f, carry):
                x = src_ref[f]
                pieces = [pltpu.roll(x, sh, 1)[:, :length] if sh else x[:, :length] for sh in shifts]
                patches = jnp.concatenate(pieces, axis=0)
                acc = jnp.dot(wsp_ref[block], patches, preferred_element_type=jnp.float32)
                s_ref[f] = acc.astype(jnp.bfloat16)
                return carry
            lax.fori_loop(0, n, body, 0)

        def temporal(block, src_ref, k):
            stacked = jnp.concatenate([s_ref[k], s_ref[k + 1], s_ref[k + 2]], axis=0)
            acc = jnp.dot(tw_ref[block], stacked, preferred_element_type=jnp.float32) + tb_ref[block]
            centre = src_ref[k + 2, :, base:base + length].astype(jnp.float32)
            return (centre + jnp.maximum(acc, 0.0)).astype(jnp.bfloat16)

        spatial(0, ha_ref, n_in)

        def block0(k, carry):
            h1 = temporal(0, ha_ref, k)
            keep = mask1 & (first + 2 + k >= 0)
            hb2_ref[k, :, base:base + length] = jnp.where(keep, h1, jnp.zeros_like(h1))
            return carry

        lax.fori_loop(0, n_in - 2, block0, 0)
        spatial(1, hb2_ref, n_in - 2)

        def block1(k, carry):
            h2 = temporal(1, hb2_ref, k).astype(jnp.float32)
            head = jnp.sum(hw_ref[...] * h2, axis=0, keepdims=True) + hb_ref[...]
            out_ref[k] = head
            return carry

        lax.fori_loop(0, count, block1, 0)

    return kernel


def shards(video, stem_weight, stem_bias, spatial_weight, temporal_weight, temporal_bias, head_weight, head_bias):
    clip = video[:, 0]
    count, height, width = clip.shape
    lead = shifted(clip[-LEAD:], "tm", 1)
    extended = spread(jnp.concatenate([lead, clip], axis=0), HALO)
    n_in = count + LEAD
    pitch = width + 2 * HALO
    rows = height + 2 * HALO
    length = round_up(rows * pitch, 128)
    base = round_up(pitch + 1, 128)
    total = length + 2 * base
    flat = extended.reshape(n_in, rows * pitch)
    flat = jnp.pad(flat.astype(jnp.float32), ((0, 0), (base, total - base - rows * pitch)))
    vp = flat[:, None, :]

    channels = stem_weight.shape[1]
    w_hi = stem_weight.astype(jnp.bfloat16)
    w_lo = (stem_weight - w_hi.astype(jnp.float32)).astype(jnp.bfloat16)
    wst = jnp.zeros((channels, 32), jnp.bfloat16)
    wst = wst.at[:, 0:9].set(w_hi.T).at[:, 16:25].set(w_lo.T)
    bst = stem_bias.astype(jnp.float32)[:, None]
    wsp = spatial_weight.transpose(0, 2, 1, 3).reshape(2, channels, 9 * channels)
    tw = temporal_weight.transpose(0, 2, 1, 3).reshape(2, channels, 3 * channels)
    tb = temporal_bias.astype(jnp.float32)[:, :, None]
    hw = head_weight.astype(jnp.float32)[:, None]
    hb = head_bias.astype(jnp.float32).reshape(1, 1)
    masks = flat_masks(height, width, length)
    first = (lax.axis_index("tm") * count - LEAD).astype(jnp.int32).reshape(1)

    vmem = pltpu.MemorySpace.VMEM if hasattr(pltpu, "MemorySpace") else pltpu.TPUMemorySpace.VMEM
    smem = pltpu.MemorySpace.SMEM if hasattr(pltpu, "MemorySpace") else pltpu.TPUMemorySpace.SMEM
    spec = pl.BlockSpec(memory_space=vmem)
    out = pl.pallas_call(
        make_kernel(n_in, count, pitch, length, base, total),
        out_shape=jax.ShapeDtypeStruct((count, 1, length), jnp.float32),
        in_specs=[pl.BlockSpec(memory_space=smem)] + [spec] * 9,
        out_specs=spec,
        scratch_shapes=[
            pltpu.VMEM((n_in, channels, total), jnp.bfloat16),
            pltpu.VMEM((n_in - 2, channels, total), jnp.bfloat16),
            pltpu.VMEM((n_in, channels, length), jnp.bfloat16),
        ],
        compiler_params=pltpu.CompilerParams(vmem_limit_bytes=48 * 1024 * 1024),
    )(first, vp, masks, wst, bst, wsp, tw, tb, hw, hb)
    result = out[:, 0, : rows * pitch].reshape(count, rows, pitch)
    result = result[:, HALO:HALO + height, HALO:HALO + width]
    return result[:, None]


def solution(mesh):
    placed = (P("tm", "space", None, None), P(), P(), P(), P(), P(), P(), P())
    return jax.shard_map(
        shards, mesh=mesh, in_specs=placed, out_specs=P("tm", "space", None, None), check_vma=False
    )
```

```python
import jax
import jax.numpy as jnp
from jax import lax
from jax.experimental import pallas as pl
from jax.experimental.pallas import tpu as pltpu
from jax.sharding import PartitionSpec as P

HALO = 3
LEAD = 4


def shifted(value, axis, steps):
    count = lax.axis_size(axis)
    leading, last = (max(0, -steps), min(count, count - steps))
    if leading >= last:
        return jnp.zeros_like(value)
    return lax.ppermute(value, axis, [(source, source + steps) for source in range(leading, last)])


def grid_shape():
    parts = lax.axis_size("space")
    grid_w = min(4, parts)
    return parts // grid_w, grid_w


def spread(field, width):
    grid_w = grid_shape()[1]
    column = lax.axis_index("space") % grid_w
    west_piece = field[..., -width:]
    east_piece = field[..., :width]
    west_piece = jnp.where(column < grid_w - 1, west_piece, jnp.zeros_like(west_piece))
    east_piece = jnp.where(column > 0, east_piece, jnp.zeros_like(east_piece))
    west = shifted(west_piece, "space", 1)
    east = shifted(east_piece, "space", -1)
    wide = jnp.concatenate([west, field, east], axis=-1)
    north = shifted(wide[..., -width:, :], "space", grid_w)
    south = shifted(wide[..., :width, :], "space", -grid_w)
    return jnp.concatenate([north, wide, south], axis=-2)


def round_up(value, step):
    return (value + step - 1) // step * step


def flat_masks(height, width, length):
    grid_h, grid_w = grid_shape()
    place = lax.axis_index("space")
    pitch = width + 2 * HALO
    q = jnp.arange(length)
    y = q // pitch - HALO
    x = q % pitch - HALO
    gy = place // grid_w * height + y
    gx = place % grid_w * width + x
    inside = (q < (height + 2 * HALO) * pitch) & (gy >= 0) & (gy < grid_h * height)
    inside = inside & (gx >= 0) & (gx < grid_w * width)
    rows = []
    for margin in (2, 1):
        keep = inside & (y >= -margin) & (y < height + margin) & (x >= -margin) & (x < width + margin)
        rows.append(keep.astype(jnp.float32))
    return jnp.stack(rows)[:, None, :]


def make_kernel(n_in, count, pitch, length, base, total, height):
    offs = [(dy - 1) * pitch + (dx - 1) for dy in range(3) for dx in range(3)]
    shifts = [(-(base + off)) % total for off in offs]

    def span(margin):
        lo = (HALO - margin) * pitch // 128 * 128
        hi = min(length, round_up((HALO + height + margin) * pitch, 128))
        return lo, hi

    spans = [span(2), span(1), span(0)]

    def kernel(first_ref, vp_ref, mask_ref, wst_ref, bst_ref, wsp_ref, tw_ref, tb_ref, hw_ref, hb_ref,
               out_ref, ha_ref, hb2_ref, s_ref):
        first = first_ref[0]
        channels = ha_ref.shape[1]

        def clear(ref, n, lo, hi):
            front = jnp.zeros((channels, base + lo), jnp.bfloat16)
            back = jnp.zeros((channels, total - base - hi), jnp.bfloat16)

            def body(f, carry):
                ref[f, :, 0:base + lo] = front
                ref[f, :, base + hi:total] = back
                return carry
            lax.fori_loop(0, n, body, 0)

        clear(ha_ref, n_in, *spans[0])
        clear(hb2_ref, n_in - 2, *spans[1])

        lo0, hi0 = spans[0]
        mask0 = mask_ref[0, :, lo0:hi0] > 0.5
        filler = jnp.zeros((16 - len(shifts), hi0 - lo0), jnp.float32)

        def stem(f, carry):
            v = vp_ref[f]
            rows = [pltpu.roll(v, sh, 1)[:, lo0:hi0] if sh else v[:, lo0:hi0] for sh in shifts]
            patch = jnp.concatenate(rows + [filler], axis=0).astype(jnp.bfloat16)
            patch = jnp.concatenate([patch, patch], axis=0)
            acc = jnp.dot(wst_ref[...], patch, preferred_element_type=jnp.float32)
            h0 = jnp.maximum(acc + bst_ref[...], 0.0).astype(jnp.bfloat16)
            keep = mask0 & (first + f >= 0)
            ha_ref[f, :, base + lo0:base + hi0] = jnp.where(keep, h0, jnp.zeros_like(h0))
            return carry

        lax.fori_loop(0, n_in, stem, 0)

        def spatial(block, src_ref, n, lo, hi):
            def body(f, carry):
                x = src_ref[f]
                pieces = [pltpu.roll(x, sh, 1)[:, lo:hi] if sh else x[:, lo:hi] for sh in shifts]
                patches = jnp.concatenate(pieces, axis=0)
                acc = jnp.dot(wsp_ref[block], patches, preferred_element_type=jnp.float32)
                s_ref[f, :, lo:hi] = acc.astype(jnp.bfloat16)
                return carry
            lax.fori_loop(0, n, body, 0)

        def temporal(block, src_ref, k, lo, hi):
            stacked = jnp.concatenate([s_ref[k, :, lo:hi], s_ref[k + 1, :, lo:hi], s_ref[k + 2, :, lo:hi]], axis=0)
            acc = jnp.dot(tw_ref[block], stacked, preferred_element_type=jnp.float32) + tb_ref[block]
            centre = src_ref[k + 2, :, base + lo:base + hi].astype(jnp.float32)
            return (centre + jnp.maximum(acc, 0.0)).astype(jnp.bfloat16)

        lo1, hi1 = spans[1]
        spatial(0, ha_ref, n_in, lo1, hi1)
        mask1 = mask_ref[1, :, lo1:hi1] > 0.5

        def block0(k, carry):
            h1 = temporal(0, ha_ref, k, lo1, hi1)
            keep = mask1 & (first + 2 + k >= 0)
            hb2_ref[k, :, base + lo1:base + hi1] = jnp.where(keep, h1, jnp.zeros_like(h1))
            return carry

        lax.fori_loop(0, n_in - 2, block0, 0)
        lo2, hi2 = spans[2]
        spatial(1, hb2_ref, n_in - 2, lo2, hi2)

        def block1(k, carry):
            h2 = temporal(1, hb2_ref, k, lo2, hi2).astype(jnp.float32)
            head = jnp.sum(hw_ref[...] * h2, axis=0, keepdims=True) + hb_ref[...]
            out_ref[k, :, lo2:hi2] = head
            return carry

        lax.fori_loop(0, count, block1, 0)

    return kernel


def shards(video, stem_weight, stem_bias, spatial_weight, temporal_weight, temporal_bias, head_weight, head_bias):
    clip = video[:, 0]
    count, height, width = clip.shape
    lead = shifted(clip[-LEAD:], "tm", 1)
    extended = spread(jnp.concatenate([lead, clip], axis=0), HALO)
    n_in = count + LEAD
    pitch = width + 2 * HALO
    rows = height + 2 * HALO
    length = round_up(rows * pitch, 128)
    base = round_up(pitch + 1, 128)
    total = length + 2 * base
    flat = extended.reshape(n_in, rows * pitch)
    flat = jnp.pad(flat.astype(jnp.float32), ((0, 0), (base, total - base - rows * pitch)))
    vp = flat[:, None, :]

    channels = stem_weight.shape[1]
    w_hi = stem_weight.astype(jnp.bfloat16)
    w_lo = (stem_weight - w_hi.astype(jnp.float32)).astype(jnp.bfloat16)
    wst = jnp.zeros((channels, 32), jnp.bfloat16)
    wst = wst.at[:, 0:9].set(w_hi.T).at[:, 16:25].set(w_lo.T)
    bst = stem_bias.astype(jnp.float32)[:, None]
    wsp = spatial_weight.transpose(0, 2, 1, 3).reshape(2, channels, 9 * channels)
    tw = temporal_weight.transpose(0, 2, 1, 3).reshape(2, channels, 3 * channels)
    tb = temporal_bias.astype(jnp.float32)[:, :, None]
    hw = head_weight.astype(jnp.float32)[:, None]
    hb = head_bias.astype(jnp.float32).reshape(1, 1)
    masks = flat_masks(height, width, length)
    first = (lax.axis_index("tm") * count - LEAD).astype(jnp.int32).reshape(1)

    vmem = pltpu.MemorySpace.VMEM if hasattr(pltpu, "MemorySpace") else pltpu.TPUMemorySpace.VMEM
    smem = pltpu.MemorySpace.SMEM if hasattr(pltpu, "MemorySpace") else pltpu.TPUMemorySpace.SMEM
    spec = pl.BlockSpec(memory_space=vmem)
    out = pl.pallas_call(
        make_kernel(n_in, count, pitch, length, base, total, height),
        out_shape=jax.ShapeDtypeStruct((count, 1, length), jnp.float32),
        in_specs=[pl.BlockSpec(memory_space=smem)] + [spec] * 9,
        out_specs=spec,
        scratch_shapes=[
            pltpu.VMEM((n_in, channels, total), jnp.bfloat16),
            pltpu.VMEM((n_in - 2, channels, total), jnp.bfloat16),
            pltpu.VMEM((n_in, channels, length), jnp.bfloat16),
        ],
        compiler_params=pltpu.CompilerParams(vmem_limit_bytes=48 * 1024 * 1024),
    )(first, vp, masks, wst, bst, wsp, tw, tb, hw, hb)
    result = out[:, 0, : rows * pitch].reshape(count, rows, pitch)
    result = result[:, HALO:HALO + height, HALO:HALO + width]
    return result[:, None]


def solution(mesh):
    placed = (P("tm", "space", None, None), P(), P(), P(), P(), P(), P(), P())
    return jax.shard_map(
        shards, mesh=mesh, in_specs=placed, out_specs=P("tm", "space", None, None), check_vma=False
    )
```

```python
import jax
import jax.numpy as jnp
from jax import lax
from jax.experimental import pallas as pl
from jax.experimental.pallas import tpu as pltpu
from jax.sharding import PartitionSpec as P

HALO = 3
LEAD = 4


def shifted(value, axis, steps):
    count = lax.axis_size(axis)
    leading, last = (max(0, -steps), min(count, count - steps))
    if leading >= last:
        return jnp.zeros_like(value)
    return lax.ppermute(value, axis, [(source, source + steps) for source in range(leading, last)])


def grid_shape():
    parts = lax.axis_size("space")
    grid_w = min(4, parts)
    return parts // grid_w, grid_w


def spread(field, width):
    grid_w = grid_shape()[1]
    column = lax.axis_index("space") % grid_w
    west_piece = field[..., -width:]
    east_piece = field[..., :width]
    west_piece = jnp.where(column < grid_w - 1, west_piece, jnp.zeros_like(west_piece))
    east_piece = jnp.where(column > 0, east_piece, jnp.zeros_like(east_piece))
    west = shifted(west_piece, "space", 1)
    east = shifted(east_piece, "space", -1)
    wide = jnp.concatenate([west, field, east], axis=-1)
    north = shifted(wide[..., -width:, :], "space", grid_w)
    south = shifted(wide[..., :width, :], "space", -grid_w)
    return jnp.concatenate([north, wide, south], axis=-2)


def round_up(value, step):
    return (value + step - 1) // step * step


def flat_masks(height, width, length):
    grid_h, grid_w = grid_shape()
    place = lax.axis_index("space")
    pitch = width + 2 * HALO
    q = jnp.arange(length)
    y = q // pitch - HALO
    x = q % pitch - HALO
    gy = place // grid_w * height + y
    gx = place % grid_w * width + x
    inside = (q < (height + 2 * HALO) * pitch) & (gy >= 0) & (gy < grid_h * height)
    inside = inside & (gx >= 0) & (gx < grid_w * width)
    rows = []
    for margin in (2, 1):
        keep = inside & (y >= -margin) & (y < height + margin) & (x >= -margin) & (x < width + margin)
        rows.append(keep.astype(jnp.float32))
    return jnp.stack(rows)[:, None, :]


def make_kernel(n_in, count, pitch, length, base, total, height):
    offs = [(dy - 1) * pitch + (dx - 1) for dy in range(3) for dx in range(3)]
    shifts = [(-(base + off)) % total for off in offs]

    def span(margin):
        lo = (HALO - margin) * pitch // 128 * 128
        hi = min(length, round_up((HALO + height + margin) * pitch, 128))
        return lo, hi

    spans = [span(2), span(1), span(0)]

    def kernel(first_ref, vp_ref, mask_ref, wst_ref, bst_ref, wsp_ref, tw_ref, tb_ref, hw_ref, hb_ref,
               out_ref, ha_ref, hb2_ref, s_ref):
        first = first_ref[0]
        channels = ha_ref.shape[1]

        def clear(ref, n, lo, hi):
            front = jnp.zeros((channels, base + lo), jnp.bfloat16)
            back = jnp.zeros((channels, total - base - hi), jnp.bfloat16)

            def body(f, carry):
                ref[f, :, 0:base + lo] = front
                ref[f, :, base + hi:total] = back
                return carry
            lax.fori_loop(0, n, body, 0)

        clear(ha_ref, n_in, *spans[0])
        clear(hb2_ref, n_in - 2, *spans[1])

        lo0, hi0 = spans[0]
        mask0 = mask_ref[0, :, lo0:hi0] > 0.5
        filler = jnp.zeros((16 - len(shifts), hi0 - lo0), jnp.float32)

        def stem(f, carry):
            v = vp_ref[f]
            rows = [pltpu.roll(v, sh, 1)[:, lo0:hi0] if sh else v[:, lo0:hi0] for sh in shifts]
            patch = jnp.concatenate(rows + [filler], axis=0).astype(jnp.bfloat16)
            patch = jnp.concatenate([patch, patch], axis=0)
            acc = jnp.dot(wst_ref[...], patch, preferred_element_type=jnp.float32)
            h0 = jnp.maximum(acc + bst_ref[...], 0.0).astype(jnp.bfloat16)
            keep = mask0 & (first + f >= 0)
            ha_ref[f, :, base + lo0:base + hi0] = jnp.where(keep, h0, jnp.zeros_like(h0))
            return carry

        lax.fori_loop(0, n_in, stem, 0)

        def spatial(block, src_ref, n, wide, lo, hi):
            lo_y, hi_y = wide
            width_y = hi_y - lo_y
            dx_shifts = [(-(base + dx - 1)) % total for dx in range(3)]

            def body(f, carry):
                x = src_ref[f]
                pieces = [pltpu.roll(x, sh, 1)[:, lo_y:hi_y] for sh in dx_shifts]
                patches = jnp.concatenate(pieces, axis=0)
                y = jnp.dot(wsp_ref[block], patches, preferred_element_type=jnp.float32)
                a, b = lo - lo_y, hi - lo_y
                up = pltpu.roll(y[0:channels], pitch, 1)[:, a:b]
                down = pltpu.roll(y[2 * channels:3 * channels], width_y - pitch, 1)[:, a:b]
                acc = up + y[channels:2 * channels, a:b] + down
                s_ref[f, :, lo:hi] = acc.astype(jnp.bfloat16)
                return carry
            lax.fori_loop(0, n, body, 0)

        def temporal(block, src_ref, k, lo, hi):
            stacked = jnp.concatenate([s_ref[k, :, lo:hi], s_ref[k + 1, :, lo:hi], s_ref[k + 2, :, lo:hi]], axis=0)
            acc = jnp.dot(tw_ref[block], stacked, preferred_element_type=jnp.float32) + tb_ref[block]
            centre = src_ref[k + 2, :, base + lo:base + hi].astype(jnp.float32)
            return (centre + jnp.maximum(acc, 0.0)).astype(jnp.bfloat16)

        lo1, hi1 = spans[1]
        spatial(0, ha_ref, n_in, spans[0], lo1, hi1)
        mask1 = mask_ref[1, :, lo1:hi1] > 0.5

        def block0(k, carry):
            h1 = temporal(0, ha_ref, k, lo1, hi1)
            keep = mask1 & (first + 2 + k >= 0)
            hb2_ref[k, :, base + lo1:base + hi1] = jnp.where(keep, h1, jnp.zeros_like(h1))
            return carry

        lax.fori_loop(0, n_in - 2, block0, 0)
        lo2, hi2 = spans[2]
        spatial(1, hb2_ref, n_in - 2, spans[1], lo2, hi2)

        def block1(k, carry):
            h2 = temporal(1, hb2_ref, k, lo2, hi2).astype(jnp.float32)
            head = jnp.sum(hw_ref[...] * h2, axis=0, keepdims=True) + hb_ref[...]
            out_ref[k, :, lo2:hi2] = head
            return carry

        lax.fori_loop(0, count, block1, 0)

    return kernel


def shards(video, stem_weight, stem_bias, spatial_weight, temporal_weight, temporal_bias, head_weight, head_bias):
    clip = video[:, 0]
    count, height, width = clip.shape
    lead = shifted(clip[-LEAD:], "tm", 1)
    extended = spread(jnp.concatenate([lead, clip], axis=0), HALO)
    n_in = count + LEAD
    pitch = width + 2 * HALO
    rows = height + 2 * HALO
    length = round_up(rows * pitch, 128)
    base = round_up(pitch + 1, 128)
    total = length + 2 * base
    flat = extended.reshape(n_in, rows * pitch)
    flat = jnp.pad(flat.astype(jnp.float32), ((0, 0), (base, total - base - rows * pitch)))
    vp = flat[:, None, :]

    channels = stem_weight.shape[1]
    w_hi = stem_weight.astype(jnp.bfloat16)
    w_lo = (stem_weight - w_hi.astype(jnp.float32)).astype(jnp.bfloat16)
    wst = jnp.zeros((channels, 32), jnp.bfloat16)
    wst = wst.at[:, 0:9].set(w_hi.T).at[:, 16:25].set(w_lo.T)
    bst = stem_bias.astype(jnp.float32)[:, None]
    wsp = spatial_weight.reshape(2, 3, 3, channels, channels).transpose(0, 1, 3, 2, 4)
    wsp = wsp.reshape(2, 3 * channels, 3 * channels)
    tw = temporal_weight.transpose(0, 2, 1, 3).reshape(2, channels, 3 * channels)
    tb = temporal_bias.astype(jnp.float32)[:, :, None]
    hw = head_weight.astype(jnp.float32)[:, None]
    hb = head_bias.astype(jnp.float32).reshape(1, 1)
    masks = flat_masks(height, width, length)
    first = (lax.axis_index("tm") * count - LEAD).astype(jnp.int32).reshape(1)

    vmem = pltpu.MemorySpace.VMEM if hasattr(pltpu, "MemorySpace") else pltpu.TPUMemorySpace.VMEM
    smem = pltpu.MemorySpace.SMEM if hasattr(pltpu, "MemorySpace") else pltpu.TPUMemorySpace.SMEM
    spec = pl.BlockSpec(memory_space=vmem)
    out = pl.pallas_call(
        make_kernel(n_in, count, pitch, length, base, total, height),
        out_shape=jax.ShapeDtypeStruct((count, 1, length), jnp.float32),
        in_specs=[pl.BlockSpec(memory_space=smem)] + [spec] * 9,
        out_specs=spec,
        scratch_shapes=[
            pltpu.VMEM((n_in, channels, total), jnp.bfloat16),
            pltpu.VMEM((n_in - 2, channels, total), jnp.bfloat16),
            pltpu.VMEM((n_in, channels, length), jnp.bfloat16),
        ],
        compiler_params=pltpu.CompilerParams(vmem_limit_bytes=48 * 1024 * 1024),
    )(first, vp, masks, wst, bst, wsp, tw, tb, hw, hb)
    result = out[:, 0, : rows * pitch].reshape(count, rows, pitch)
    result = result[:, HALO:HALO + height, HALO:HALO + width]
    return result[:, None]


def solution(mesh):
    placed = (P("tm", "space", None, None), P(), P(), P(), P(), P(), P(), P())
    return jax.shard_map(
        shards, mesh=mesh, in_specs=placed, out_specs=P("tm", "space", None, None), check_vma=False
    )
```

```python
import jax
import jax.numpy as jnp
from jax import lax
from jax.experimental import pallas as pl
from jax.experimental.pallas import tpu as pltpu
from jax.sharding import PartitionSpec as P

HALO = 3
LEAD = 4


def shifted(value, axis, steps):
    count = lax.axis_size(axis)
    leading, last = (max(0, -steps), min(count, count - steps))
    if leading >= last:
        return jnp.zeros_like(value)
    return lax.ppermute(value, axis, [(source, source + steps) for source in range(leading, last)])


def grid_shape():
    parts = lax.axis_size("space")
    grid_w = min(4, parts)
    return parts // grid_w, grid_w


def spread(field, width):
    grid_w = grid_shape()[1]
    column = lax.axis_index("space") % grid_w
    west_piece = field[..., -width:]
    east_piece = field[..., :width]
    west_piece = jnp.where(column < grid_w - 1, west_piece, jnp.zeros_like(west_piece))
    east_piece = jnp.where(column > 0, east_piece, jnp.zeros_like(east_piece))
    west = shifted(west_piece, "space", 1)
    east = shifted(east_piece, "space", -1)
    wide = jnp.concatenate([west, field, east], axis=-1)
    north = shifted(wide[..., -width:, :], "space", grid_w)
    south = shifted(wide[..., :width, :], "space", -grid_w)
    return jnp.concatenate([north, wide, south], axis=-2)


def round_up(value, step):
    return (value + step - 1) // step * step


def flat_masks(height, width, length):
    grid_h, grid_w = grid_shape()
    place = lax.axis_index("space")
    pitch = width + 2 * HALO
    q = jnp.arange(length)
    y = q // pitch - HALO
    x = q % pitch - HALO
    gy = place // grid_w * height + y
    gx = place % grid_w * width + x
    inside = (q < (height + 2 * HALO) * pitch) & (gy >= 0) & (gy < grid_h * height)
    inside = inside & (gx >= 0) & (gx < grid_w * width)
    rows = []
    for margin in (2, 1):
        keep = inside & (y >= -margin) & (y < height + margin) & (x >= -margin) & (x < width + margin)
        rows.append(keep.astype(jnp.float32))
    return jnp.stack(rows)[:, None, :]


def make_kernel(n_in, count, pitch, length, base, total, height):
    offs = [(dy - 1) * pitch + (dx - 1) for dy in range(3) for dx in range(3)]
    shifts = [(-(base + off)) % total for off in offs]

    def span(margin):
        lo = (HALO - margin) * pitch // 128 * 128
        hi = min(length, round_up((HALO + height + margin) * pitch, 128))
        return lo, hi

    spans = [span(2), span(1), span(0)]

    def kernel(first_ref, vp_ref, mask_ref, wst_ref, bst_ref, wsp_ref, tw_ref, tb_ref, hw_ref, hb_ref,
               out_ref, ha_ref, hb2_ref, s_ref):
        first = first_ref[0]
        channels = ha_ref.shape[1]

        def clear(ref, n, lo, hi):
            front = jnp.zeros((channels, base + lo), jnp.bfloat16)
            back = jnp.zeros((channels, total - base - hi), jnp.bfloat16)

            def body(f, carry):
                ref[f, :, 0:base + lo] = front
                ref[f, :, base + hi:total] = back
                return carry
            lax.fori_loop(0, n, body, 0)

        clear(ha_ref, n_in, *spans[0])
        clear(hb2_ref, n_in - 2, *spans[1])

        lo0, hi0 = spans[0]
        mask0 = mask_ref[0, :, lo0:hi0] > 0.5
        group = 8
        filler = jnp.zeros((group, hi0 - lo0), jnp.float32)
        for g in range(vp_ref.shape[0] // group):
            v = vp_ref[g * group:(g + 1) * group, :]
            rows = [pltpu.roll(v, sh, 1)[:, lo0:hi0] if sh else v[:, lo0:hi0] for sh in shifts]
            patch = jnp.concatenate(rows + [filler], axis=0).astype(jnp.bfloat16)
            patch = jnp.concatenate([patch, patch], axis=0)
            acc = jnp.dot(wst_ref[...], patch, preferred_element_type=jnp.float32)
            for j in range(group):
                f = g * group + j
                if f >= n_in:
                    break
                part = acc[j * channels:(j + 1) * channels]
                h0 = jnp.maximum(part + bst_ref[...], 0.0).astype(jnp.bfloat16)
                keep = mask0 & (first + f >= 0)
                ha_ref[f, :, base + lo0:base + hi0] = jnp.where(keep, h0, jnp.zeros_like(h0))

        def spatial(block, src_ref, n, wide, lo, hi):
            lo_y, hi_y = wide
            width_y = hi_y - lo_y
            dx_shifts = [(-(base + dx - 1)) % total for dx in range(3)]

            def body(f, carry):
                x = src_ref[f]
                pieces = [pltpu.roll(x, sh, 1)[:, lo_y:hi_y] for sh in dx_shifts]
                patches = jnp.concatenate(pieces, axis=0)
                y = jnp.dot(wsp_ref[block], patches, preferred_element_type=jnp.float32)
                a, b = lo - lo_y, hi - lo_y
                up = pltpu.roll(y[0:channels], pitch, 1)[:, a:b]
                down = pltpu.roll(y[2 * channels:3 * channels], width_y - pitch, 1)[:, a:b]
                acc = up + y[channels:2 * channels, a:b] + down
                s_ref[f, :, lo:hi] = acc.astype(jnp.bfloat16)
                return carry
            lax.fori_loop(0, n, body, 0)

        def temporal(block, src_ref, k, lo, hi):
            stacked = jnp.concatenate([s_ref[k, :, lo:hi], s_ref[k + 1, :, lo:hi], s_ref[k + 2, :, lo:hi]], axis=0)
            acc = jnp.dot(tw_ref[block], stacked, preferred_element_type=jnp.float32) + tb_ref[block]
            centre = src_ref[k + 2, :, base + lo:base + hi].astype(jnp.float32)
            return (centre + jnp.maximum(acc, 0.0)).astype(jnp.bfloat16)

        lo1, hi1 = spans[1]
        spatial(0, ha_ref, n_in, spans[0], lo1, hi1)
        mask1 = mask_ref[1, :, lo1:hi1] > 0.5

        def block0(k, carry):
            h1 = temporal(0, ha_ref, k, lo1, hi1)
            keep = mask1 & (first + 2 + k >= 0)
            hb2_ref[k, :, base + lo1:base + hi1] = jnp.where(keep, h1, jnp.zeros_like(h1))
            return carry

        lax.fori_loop(0, n_in - 2, block0, 0)
        lo2, hi2 = spans[2]
        spatial(1, hb2_ref, n_in - 2, spans[1], lo2, hi2)

        def block1(k, carry):
            h2 = temporal(1, hb2_ref, k, lo2, hi2).astype(jnp.float32)
            head = jnp.sum(hw_ref[...] * h2, axis=0, keepdims=True) + hb_ref[...]
            out_ref[k, :, lo2:hi2] = head
            return carry

        lax.fori_loop(0, count, block1, 0)

    return kernel


def shards(video, stem_weight, stem_bias, spatial_weight, temporal_weight, temporal_bias, head_weight, head_bias):
    clip = video[:, 0]
    count, height, width = clip.shape
    lead = shifted(clip[-LEAD:], "tm", 1)
    extended = spread(jnp.concatenate([lead, clip], axis=0), HALO)
    n_in = count + LEAD
    pitch = width + 2 * HALO
    rows = height + 2 * HALO
    length = round_up(rows * pitch, 128)
    base = round_up(pitch + 1, 128)
    total = length + 2 * base
    flat = extended.reshape(n_in, rows * pitch)
    n_pad = round_up(n_in, 8)
    flat = jnp.pad(flat.astype(jnp.float32), ((0, n_pad - n_in), (base, total - base - rows * pitch)))
    vp = flat

    channels = stem_weight.shape[1]
    w_hi = stem_weight.astype(jnp.bfloat16).astype(jnp.float32)
    w_lo = stem_weight - w_hi
    eye = jnp.eye(8, dtype=jnp.float32)

    def spread_taps(w):
        w = jnp.pad(w, ((0, 1), (0, 0)))
        return jnp.einsum("to,jk->jotk", w, eye).reshape(8 * channels, 8 * w.shape[0])

    wst = jnp.concatenate([spread_taps(w_hi), spread_taps(w_lo)], axis=1).astype(jnp.bfloat16)
    bst = stem_bias.astype(jnp.float32)[:, None]
    wsp = spatial_weight.reshape(2, 3, 3, channels, channels).transpose(0, 1, 3, 2, 4)
    wsp = wsp.reshape(2, 3 * channels, 3 * channels)
    tw = temporal_weight.transpose(0, 2, 1, 3).reshape(2, channels, 3 * channels)
    tb = temporal_bias.astype(jnp.float32)[:, :, None]
    hw = head_weight.astype(jnp.float32)[:, None]
    hb = head_bias.astype(jnp.float32).reshape(1, 1)
    masks = flat_masks(height, width, length)
    first = (lax.axis_index("tm") * count - LEAD).astype(jnp.int32).reshape(1)

    vmem = pltpu.MemorySpace.VMEM if hasattr(pltpu, "MemorySpace") else pltpu.TPUMemorySpace.VMEM
    smem = pltpu.MemorySpace.SMEM if hasattr(pltpu, "MemorySpace") else pltpu.TPUMemorySpace.SMEM
    spec = pl.BlockSpec(memory_space=vmem)
    out = pl.pallas_call(
        make_kernel(n_in, count, pitch, length, base, total, height),
        out_shape=jax.ShapeDtypeStruct((count, 1, length), jnp.float32),
        in_specs=[pl.BlockSpec(memory_space=smem)] + [spec] * 9,
        out_specs=spec,
        scratch_shapes=[
            pltpu.VMEM((n_in, channels, total), jnp.bfloat16),
            pltpu.VMEM((n_in - 2, channels, total), jnp.bfloat16),
            pltpu.VMEM((n_in, channels, length), jnp.bfloat16),
        ],
        compiler_params=pltpu.CompilerParams(vmem_limit_bytes=48 * 1024 * 1024),
    )(first, vp, masks, wst, bst, wsp, tw, tb, hw, hb)
    result = out[:, 0, : rows * pitch].reshape(count, rows, pitch)
    result = result[:, HALO:HALO + height, HALO:HALO + width]
    return result[:, None]


def solution(mesh):
    placed = (P("tm", "space", None, None), P(), P(), P(), P(), P(), P(), P())
    return jax.shard_map(
        shards, mesh=mesh, in_specs=placed, out_specs=P("tm", "space", None, None), check_vma=False
    )
```

```python
import jax
import jax.numpy as jnp
from jax import lax
from jax.experimental import pallas as pl
from jax.experimental.pallas import tpu as pltpu
from jax.sharding import PartitionSpec as P

HALO = 3
LEAD = 4


def shifted(value, axis, steps):
    count = lax.axis_size(axis)
    leading, last = (max(0, -steps), min(count, count - steps))
    if leading >= last:
        return jnp.zeros_like(value)
    return lax.ppermute(value, axis, [(source, source + steps) for source in range(leading, last)])


def grid_shape():
    parts = lax.axis_size("space")
    grid_w = min(4, parts)
    return parts // grid_w, grid_w


def spread(field, width):
    grid_w = grid_shape()[1]
    column = lax.axis_index("space") % grid_w
    west_piece = field[..., -width:]
    east_piece = field[..., :width]
    west_piece = jnp.where(column < grid_w - 1, west_piece, jnp.zeros_like(west_piece))
    east_piece = jnp.where(column > 0, east_piece, jnp.zeros_like(east_piece))
    west = shifted(west_piece, "space", 1)
    east = shifted(east_piece, "space", -1)
    wide = jnp.concatenate([west, field, east], axis=-1)
    north = shifted(wide[..., -width:, :], "space", grid_w)
    south = shifted(wide[..., :width, :], "space", -grid_w)
    return jnp.concatenate([north, wide, south], axis=-2)


def round_up(value, step):
    return (value + step - 1) // step * step


def flat_masks(height, width, length):
    grid_h, grid_w = grid_shape()
    place = lax.axis_index("space")
    pitch = width + 2 * HALO
    q = jnp.arange(length)
    y = q // pitch - HALO
    x = q % pitch - HALO
    gy = place // grid_w * height + y
    gx = place % grid_w * width + x
    inside = (q < (height + 2 * HALO) * pitch) & (gy >= 0) & (gy < grid_h * height)
    inside = inside & (gx >= 0) & (gx < grid_w * width)
    rows = []
    for margin in (2, 1):
        keep = inside & (y >= -margin) & (y < height + margin) & (x >= -margin) & (x < width + margin)
        rows.append(keep.astype(jnp.float32))
    return jnp.stack(rows)[:, None, :]


def make_kernel(n_in, count, pitch, length, base, total, height):
    offs = [(dy - 1) * pitch + (dx - 1) for dy in range(3) for dx in range(3)]
    shifts = [(-(base + off)) % total for off in offs]

    def span(margin):
        lo = (HALO - margin) * pitch // 128 * 128
        hi = min(length, round_up((HALO + height + margin) * pitch, 128))
        return lo, hi

    spans = [span(2), span(1), span(0)]

    def kernel(first_ref, vp_ref, mask_ref, wst_ref, bst_ref, wsp_ref, tw_ref, tb_ref, hw_ref, hb_ref,
               out_ref, ha_ref, hb2_ref, s_ref):
        first = first_ref[0]
        channels = ha_ref.shape[1]

        def clear(ref, n, lo, hi):
            front = jnp.zeros((channels, base + lo), jnp.bfloat16)
            back = jnp.zeros((channels, total - base - hi), jnp.bfloat16)

            def body(f, carry):
                ref[f, :, 0:base + lo] = front
                ref[f, :, base + hi:total] = back
                return carry
            lax.fori_loop(0, n, body, 0)

        clear(ha_ref, n_in, *spans[0])
        clear(hb2_ref, n_in - 2, *spans[1])

        lo0, hi0 = spans[0]
        mask0 = mask_ref[0, :, lo0:hi0] > 0.5
        group = 8
        filler = jnp.zeros((group, hi0 - lo0), jnp.float32)
        for g in range(vp_ref.shape[0] // group):
            v = vp_ref[g * group:(g + 1) * group, :]
            rows = [pltpu.roll(v, sh, 1)[:, lo0:hi0] if sh else v[:, lo0:hi0] for sh in shifts]
            patch = jnp.concatenate(rows + [filler], axis=0).astype(jnp.bfloat16)
            patch = jnp.concatenate([patch, patch], axis=0)
            acc = jnp.dot(wst_ref[...], patch, preferred_element_type=jnp.float32)
            for j in range(group):
                f = g * group + j
                if f >= n_in:
                    break
                part = acc[j * channels:(j + 1) * channels]
                h0 = jnp.maximum(part + bst_ref[...], 0.0).astype(jnp.bfloat16)
                keep = mask0 & (first + f >= 0)
                ha_ref[f, :, base + lo0:base + hi0] = jnp.where(keep, h0, jnp.zeros_like(h0))

        def spatial(block, src_ref, n, wide, lo, hi):
            lo_y, hi_y = wide
            width_y = hi_y - lo_y
            dx_shifts = [(-(base + dx - 1)) % total for dx in range(3)]

            def body(f, carry):
                x = src_ref[f]
                pieces = [pltpu.roll(x, sh, 1)[:, lo_y:hi_y] for sh in dx_shifts]
                patches = jnp.concatenate(pieces, axis=0)
                y = jnp.dot(wsp_ref[block], patches, preferred_element_type=jnp.float32)
                a, b = lo - lo_y, hi - lo_y
                up = pltpu.roll(y[0:channels], pitch, 1)[:, a:b]
                down = pltpu.roll(y[2 * channels:3 * channels], width_y - pitch, 1)[:, a:b]
                acc = up + y[channels:2 * channels, a:b] + down
                s_ref[f, :, lo:hi] = acc.astype(jnp.bfloat16)
                return carry
            lax.fori_loop(0, n, body, 0)

        def temporal(block, src_ref, n_out, lo, hi, finish):
            for k0 in range(0, n_out, group):
                stacked = jnp.concatenate([s_ref[k0 + jj, :, lo:hi] for jj in range(group + 2)], axis=0)
                acc = jnp.dot(tw_ref[block], stacked, preferred_element_type=jnp.float32)
                for j in range(min(group, n_out - k0)):
                    k = k0 + j
                    part = acc[j * channels:(j + 1) * channels] + tb_ref[block]
                    centre = src_ref[k + 2, :, base + lo:base + hi].astype(jnp.float32)
                    finish(k, (centre + jnp.maximum(part, 0.0)).astype(jnp.bfloat16))

        s_ref[n_in:, :, :] = jnp.zeros((s_ref.shape[0] - n_in, channels, length), jnp.bfloat16)
        lo1, hi1 = spans[1]
        spatial(0, ha_ref, n_in, spans[0], lo1, hi1)
        mask1 = mask_ref[1, :, lo1:hi1] > 0.5

        def finish0(k, h1):
            keep = mask1 & (first + 2 + k >= 0)
            hb2_ref[k, :, base + lo1:base + hi1] = jnp.where(keep, h1, jnp.zeros_like(h1))

        temporal(0, ha_ref, n_in - 2, lo1, hi1, finish0)
        lo2, hi2 = spans[2]
        spatial(1, hb2_ref, n_in - 2, spans[1], lo2, hi2)

        def finish1(k, h2):
            head = jnp.sum(hw_ref[...] * h2.astype(jnp.float32), axis=0, keepdims=True) + hb_ref[...]
            out_ref[k, :, lo2:hi2] = head

        temporal(1, hb2_ref, count, lo2, hi2, finish1)

    return kernel


def shards(video, stem_weight, stem_bias, spatial_weight, temporal_weight, temporal_bias, head_weight, head_bias):
    clip = video[:, 0]
    count, height, width = clip.shape
    lead = shifted(clip[-LEAD:], "tm", 1)
    extended = spread(jnp.concatenate([lead, clip], axis=0), HALO)
    n_in = count + LEAD
    pitch = width + 2 * HALO
    rows = height + 2 * HALO
    length = round_up(rows * pitch, 128)
    base = round_up(pitch + 1, 128)
    total = length + 2 * base
    flat = extended.reshape(n_in, rows * pitch)
    n_pad = round_up(n_in, 8)
    flat = jnp.pad(flat.astype(jnp.float32), ((0, n_pad - n_in), (base, total - base - rows * pitch)))
    vp = flat

    channels = stem_weight.shape[1]
    w_hi = stem_weight.astype(jnp.bfloat16).astype(jnp.float32)
    w_lo = stem_weight - w_hi
    eye = jnp.eye(8, dtype=jnp.float32)

    def spread_taps(w):
        w = jnp.pad(w, ((0, 1), (0, 0)))
        return jnp.einsum("to,jk->jotk", w, eye).reshape(8 * channels, 8 * w.shape[0])

    wst = jnp.concatenate([spread_taps(w_hi), spread_taps(w_lo)], axis=1).astype(jnp.bfloat16)
    bst = stem_bias.astype(jnp.float32)[:, None]
    wsp = spatial_weight.reshape(2, 3, 3, channels, channels).transpose(0, 1, 3, 2, 4)
    wsp = wsp.reshape(2, 3 * channels, 3 * channels)
    band = jnp.stack([jnp.eye(8, 10, d, dtype=jnp.float32) for d in range(3)])
    tw = jnp.einsum("dja,bdoi->bjoai", band, temporal_weight.astype(jnp.float32))
    tw = tw.reshape(2, 8 * channels, 10 * channels).astype(jnp.bfloat16)
    tb = temporal_bias.astype(jnp.float32)[:, :, None]
    hw = head_weight.astype(jnp.float32)[:, None]
    hb = head_bias.astype(jnp.float32).reshape(1, 1)
    masks = flat_masks(height, width, length)
    first = (lax.axis_index("tm") * count - LEAD).astype(jnp.int32).reshape(1)

    vmem = pltpu.MemorySpace.VMEM if hasattr(pltpu, "MemorySpace") else pltpu.TPUMemorySpace.VMEM
    smem = pltpu.MemorySpace.SMEM if hasattr(pltpu, "MemorySpace") else pltpu.TPUMemorySpace.SMEM
    spec = pl.BlockSpec(memory_space=vmem)
    out = pl.pallas_call(
        make_kernel(n_in, count, pitch, length, base, total, height),
        out_shape=jax.ShapeDtypeStruct((count, 1, length), jnp.float32),
        in_specs=[pl.BlockSpec(memory_space=smem)] + [spec] * 9,
        out_specs=spec,
        scratch_shapes=[
            pltpu.VMEM((n_in, channels, total), jnp.bfloat16),
            pltpu.VMEM((n_in - 2, channels, total), jnp.bfloat16),
            pltpu.VMEM((round_up(n_in - 2, 8) + 2, channels, length), jnp.bfloat16),
        ],
        compiler_params=pltpu.CompilerParams(vmem_limit_bytes=48 * 1024 * 1024),
    )(first, vp, masks, wst, bst, wsp, tw, tb, hw, hb)
    result = out[:, 0, : rows * pitch].reshape(count, rows, pitch)
    result = result[:, HALO:HALO + height, HALO:HALO + width]
    return result[:, None]


def solution(mesh):
    placed = (P("tm", "space", None, None), P(), P(), P(), P(), P(), P(), P())
    return jax.shard_map(
        shards, mesh=mesh, in_specs=placed, out_specs=P("tm", "space", None, None), check_vma=False
    )
```

```python
import jax
import jax.numpy as jnp
from jax import lax
from jax.experimental import pallas as pl
from jax.experimental.pallas import tpu as pltpu
from jax.sharding import PartitionSpec as P

HALO = 3
LEAD = 4
SPATIAL_GROUP = 4


def shifted(value, axis, steps):
    count = lax.axis_size(axis)
    leading, last = (max(0, -steps), min(count, count - steps))
    if leading >= last:
        return jnp.zeros_like(value)
    return lax.ppermute(value, axis, [(source, source + steps) for source in range(leading, last)])


def grid_shape():
    parts = lax.axis_size("space")
    grid_w = min(4, parts)
    return parts // grid_w, grid_w


def spread(field, width):
    grid_w = grid_shape()[1]
    column = lax.axis_index("space") % grid_w
    west_piece = field[..., -width:]
    east_piece = field[..., :width]
    west_piece = jnp.where(column < grid_w - 1, west_piece, jnp.zeros_like(west_piece))
    east_piece = jnp.where(column > 0, east_piece, jnp.zeros_like(east_piece))
    west = shifted(west_piece, "space", 1)
    east = shifted(east_piece, "space", -1)
    wide = jnp.concatenate([west, field, east], axis=-1)
    north = shifted(wide[..., -width:, :], "space", grid_w)
    south = shifted(wide[..., :width, :], "space", -grid_w)
    return jnp.concatenate([north, wide, south], axis=-2)


def round_up(value, step):
    return (value + step - 1) // step * step


def flat_masks(height, width, length):
    grid_h, grid_w = grid_shape()
    place = lax.axis_index("space")
    pitch = width + 2 * HALO
    q = jnp.arange(length)
    y = q // pitch - HALO
    x = q % pitch - HALO
    gy = place // grid_w * height + y
    gx = place % grid_w * width + x
    inside = (q < (height + 2 * HALO) * pitch) & (gy >= 0) & (gy < grid_h * height)
    inside = inside & (gx >= 0) & (gx < grid_w * width)
    rows = []
    for margin in (2, 1):
        keep = inside & (y >= -margin) & (y < height + margin) & (x >= -margin) & (x < width + margin)
        rows.append(keep.astype(jnp.float32))
    return jnp.stack(rows)[:, None, :]


def make_kernel(n_in, count, pitch, length, base, total, height):
    offs = [(dy - 1) * pitch + (dx - 1) for dy in range(3) for dx in range(3)]
    shifts = [(-(base + off)) % total for off in offs]

    def span(margin):
        lo = (HALO - margin) * pitch // 128 * 128
        hi = min(length, round_up((HALO + height + margin) * pitch, 128))
        return lo, hi

    spans = [span(2), span(1), span(0)]

    def kernel(first_ref, vp_ref, mask_ref, wst_ref, bst_ref, wsp_ref, tw_ref, tb_ref, hw_ref, hb_ref,
               out_ref, ha_ref, hb2_ref, s_ref):
        first = first_ref[0]
        channels = ha_ref.shape[1]

        def clear(ref, n, lo, hi):
            front = jnp.zeros((channels, base + lo), jnp.bfloat16)
            back = jnp.zeros((channels, total - base - hi), jnp.bfloat16)

            def body(f, carry):
                ref[f, :, 0:base + lo] = front
                ref[f, :, base + hi:total] = back
                return carry
            lax.fori_loop(0, n, body, 0)

        clear(ha_ref, n_in, *spans[0])
        clear(hb2_ref, n_in - 2, *spans[1])

        lo0, hi0 = spans[0]
        mask0 = mask_ref[0, :, lo0:hi0] > 0.5
        group = 8
        filler = jnp.zeros((group, hi0 - lo0), jnp.float32)
        for g in range(vp_ref.shape[0] // group):
            v = vp_ref[g * group:(g + 1) * group, :]
            rows = [pltpu.roll(v, sh, 1)[:, lo0:hi0] if sh else v[:, lo0:hi0] for sh in shifts]
            patch = jnp.concatenate(rows + [filler], axis=0).astype(jnp.bfloat16)
            patch = jnp.concatenate([patch, patch], axis=0)
            acc = jnp.dot(wst_ref[...], patch, preferred_element_type=jnp.float32)
            for j in range(group):
                f = g * group + j
                if f >= n_in:
                    break
                part = acc[j * channels:(j + 1) * channels]
                h0 = jnp.maximum(part + bst_ref[...], 0.0).astype(jnp.bfloat16)
                keep = mask0 & (first + f >= 0)
                ha_ref[f, :, base + lo0:base + hi0] = jnp.where(keep, h0, jnp.zeros_like(h0))

        def spatial(block, src_ref, n, wide, lo, hi):
            lo_y, hi_y = wide
            width_y = hi_y - lo_y
            dx_shifts = [(-(base + dx - 1)) % total for dx in range(3)]
            a, b = lo - lo_y, hi - lo_y
            rows = 3 * channels
            for g0 in range(0, n, SPATIAL_GROUP):
                frames = [min(g0 + j, n - 1) for j in range(SPATIAL_GROUP)]
                pieces = []
                for f in frames:
                    x = src_ref[f]
                    pieces += [pltpu.roll(x, sh, 1)[:, lo_y:hi_y] for sh in dx_shifts]
                patches = jnp.concatenate(pieces, axis=0)
                y = jnp.dot(wsp_ref[block], patches, preferred_element_type=jnp.float32)
                for j in range(min(SPATIAL_GROUP, n - g0)):
                    part = y[j * rows:(j + 1) * rows]
                    up = pltpu.roll(part[0:channels], pitch, 1)[:, a:b]
                    down = pltpu.roll(part[2 * channels:3 * channels], width_y - pitch, 1)[:, a:b]
                    acc = up + part[channels:2 * channels, a:b] + down
                    s_ref[g0 + j, :, lo:hi] = acc.astype(jnp.bfloat16)

        def temporal(block, src_ref, n_out, lo, hi, finish):
            for k0 in range(0, n_out, group):
                stacked = jnp.concatenate([s_ref[k0 + jj, :, lo:hi] for jj in range(group + 2)], axis=0)
                acc = jnp.dot(tw_ref[block], stacked, preferred_element_type=jnp.float32)
                for j in range(min(group, n_out - k0)):
                    k = k0 + j
                    part = acc[j * channels:(j + 1) * channels] + tb_ref[block]
                    centre = src_ref[k + 2, :, base + lo:base + hi].astype(jnp.float32)
                    finish(k, (centre + jnp.maximum(part, 0.0)).astype(jnp.bfloat16))

        s_ref[n_in:, :, :] = jnp.zeros((s_ref.shape[0] - n_in, channels, length), jnp.bfloat16)
        lo1, hi1 = spans[1]
        spatial(0, ha_ref, n_in, spans[0], lo1, hi1)
        mask1 = mask_ref[1, :, lo1:hi1] > 0.5

        def finish0(k, h1):
            keep = mask1 & (first + 2 + k >= 0)
            hb2_ref[k, :, base + lo1:base + hi1] = jnp.where(keep, h1, jnp.zeros_like(h1))

        temporal(0, ha_ref, n_in - 2, lo1, hi1, finish0)
        lo2, hi2 = spans[2]
        spatial(1, hb2_ref, n_in - 2, spans[1], lo2, hi2)

        def finish1(k, h2):
            head = jnp.sum(hw_ref[...] * h2.astype(jnp.float32), axis=0, keepdims=True) + hb_ref[...]
            out_ref[k, :, lo2:hi2] = head

        temporal(1, hb2_ref, count, lo2, hi2, finish1)

    return kernel


def shards(video, stem_weight, stem_bias, spatial_weight, temporal_weight, temporal_bias, head_weight, head_bias):
    clip = video[:, 0]
    count, height, width = clip.shape
    lead = shifted(clip[-LEAD:], "tm", 1)
    extended = spread(jnp.concatenate([lead, clip], axis=0), HALO)
    n_in = count + LEAD
    pitch = width + 2 * HALO
    rows = height + 2 * HALO
    length = round_up(rows * pitch, 128)
    base = round_up(pitch + 1, 128)
    total = length + 2 * base
    flat = extended.reshape(n_in, rows * pitch)
    n_pad = round_up(n_in, 8)
    flat = jnp.pad(flat.astype(jnp.float32), ((0, n_pad - n_in), (base, total - base - rows * pitch)))
    vp = flat

    channels = stem_weight.shape[1]
    w_hi = stem_weight.astype(jnp.bfloat16).astype(jnp.float32)
    w_lo = stem_weight - w_hi
    eye = jnp.eye(8, dtype=jnp.float32)

    def spread_taps(w):
        w = jnp.pad(w, ((0, 1), (0, 0)))
        return jnp.einsum("to,jk->jotk", w, eye).reshape(8 * channels, 8 * w.shape[0])

    wst = jnp.concatenate([spread_taps(w_hi), spread_taps(w_lo)], axis=1).astype(jnp.bfloat16)
    bst = stem_bias.astype(jnp.float32)[:, None]
    wsp = spatial_weight.reshape(2, 3, 3, channels, channels).transpose(0, 1, 3, 2, 4)
    wsp = wsp.reshape(2, 3 * channels, 3 * channels)
    wsp = jnp.einsum("jk,bmn->bjmkn", jnp.eye(SPATIAL_GROUP, dtype=jnp.float32), wsp.astype(jnp.float32))
    wsp = wsp.reshape(2, SPATIAL_GROUP * 3 * channels, SPATIAL_GROUP * 3 * channels).astype(jnp.bfloat16)
    band = jnp.stack([jnp.eye(8, 10, d, dtype=jnp.float32) for d in range(3)])
    tw = jnp.einsum("dja,bdoi->bjoai", band, temporal_weight.astype(jnp.float32))
    tw = tw.reshape(2, 8 * channels, 10 * channels).astype(jnp.bfloat16)
    tb = temporal_bias.astype(jnp.float32)[:, :, None]
    hw = head_weight.astype(jnp.float32)[:, None]
    hb = head_bias.astype(jnp.float32).reshape(1, 1)
    masks = flat_masks(height, width, length)
    first = (lax.axis_index("tm") * count - LEAD).astype(jnp.int32).reshape(1)

    vmem = pltpu.MemorySpace.VMEM if hasattr(pltpu, "MemorySpace") else pltpu.TPUMemorySpace.VMEM
    smem = pltpu.MemorySpace.SMEM if hasattr(pltpu, "MemorySpace") else pltpu.TPUMemorySpace.SMEM
    spec = pl.BlockSpec(memory_space=vmem)
    out = pl.pallas_call(
        make_kernel(n_in, count, pitch, length, base, total, height),
        out_shape=jax.ShapeDtypeStruct((count, 1, length), jnp.float32),
        in_specs=[pl.BlockSpec(memory_space=smem)] + [spec] * 9,
        out_specs=spec,
        scratch_shapes=[
            pltpu.VMEM((n_in, channels, total), jnp.bfloat16),
            pltpu.VMEM((n_in - 2, channels, total), jnp.bfloat16),
            pltpu.VMEM((round_up(n_in - 2, 8) + 2, channels, length), jnp.bfloat16),
        ],
        compiler_params=pltpu.CompilerParams(vmem_limit_bytes=48 * 1024 * 1024),
    )(first, vp, masks, wst, bst, wsp, tw, tb, hw, hb)
    result = out[:, 0, : rows * pitch].reshape(count, rows, pitch)
    result = result[:, HALO:HALO + height, HALO:HALO + width]
    return result[:, None]


def solution(mesh):
    placed = (P("tm", "space", None, None), P(), P(), P(), P(), P(), P(), P())
    return jax.shard_map(
        shards, mesh=mesh, in_specs=placed, out_specs=P("tm", "space", None, None), check_vma=False
    )
```

```python
import jax
import jax.numpy as jnp
from jax import lax
from jax.experimental import pallas as pl
from jax.experimental.pallas import tpu as pltpu
from jax.sharding import PartitionSpec as P

HALO = 3
LEAD = 4
SPATIAL_GROUP = 4


def shifted(value, axis, steps):
    count = lax.axis_size(axis)
    leading, last = (max(0, -steps), min(count, count - steps))
    if leading >= last:
        return jnp.zeros_like(value)
    return lax.ppermute(value, axis, [(source, source + steps) for source in range(leading, last)])


def grid_shape():
    parts = lax.axis_size("space")
    grid_w = min(4, parts)
    return parts // grid_w, grid_w


def spread(field, width):
    grid_w = grid_shape()[1]
    column = lax.axis_index("space") % grid_w
    west_piece = field[..., -width:]
    east_piece = field[..., :width]
    west_piece = jnp.where(column < grid_w - 1, west_piece, jnp.zeros_like(west_piece))
    east_piece = jnp.where(column > 0, east_piece, jnp.zeros_like(east_piece))
    west = shifted(west_piece, "space", 1)
    east = shifted(east_piece, "space", -1)
    wide = jnp.concatenate([west, field, east], axis=-1)
    north = shifted(wide[..., -width:, :], "space", grid_w)
    south = shifted(wide[..., :width, :], "space", -grid_w)
    return jnp.concatenate([north, wide, south], axis=-2)


def round_up(value, step):
    return (value + step - 1) // step * step


def flat_masks(height, width, length):
    grid_h, grid_w = grid_shape()
    place = lax.axis_index("space")
    pitch = width + 2 * HALO
    q = jnp.arange(length)
    y = q // pitch - HALO
    x = q % pitch - HALO
    gy = place // grid_w * height + y
    gx = place % grid_w * width + x
    inside = (q < (height + 2 * HALO) * pitch) & (gy >= 0) & (gy < grid_h * height)
    inside = inside & (gx >= 0) & (gx < grid_w * width)
    rows = []
    for margin in (2, 1):
        keep = inside & (y >= -margin) & (y < height + margin) & (x >= -margin) & (x < width + margin)
        rows.append(keep.astype(jnp.float32))
    return jnp.stack(rows)[:, None, :]


def make_kernel(n_in, count, pitch, length, base, total, height):
    offs = [(dy - 1) * pitch + (dx - 1) for dy in range(3) for dx in range(3)]
    shifts = [(-(base + off)) % total for off in offs]

    def span(margin):
        lo = (HALO - margin) * pitch // 128 * 128
        hi = min(length, round_up((HALO + height + margin) * pitch, 128))
        return lo, hi

    spans = [span(2), span(1), span(0)]

    def kernel(first_ref, vp_ref, mask_ref, wst_ref, bst_ref, wsp_ref, tw_ref, tb_ref, hw_ref, hb_ref,
               out_ref, ha_ref, hb2_ref, s_ref):
        first = first_ref[0]
        channels = ha_ref.shape[1]

        def clear(ref, n, lo, hi):
            front = jnp.zeros((channels, base + lo), jnp.bfloat16)
            back = jnp.zeros((channels, total - base - hi), jnp.bfloat16)

            def body(f, carry):
                ref[f, :, 0:base + lo] = front
                ref[f, :, base + hi:total] = back
                return carry
            lax.fori_loop(0, n, body, 0)

        clear(ha_ref, n_in, *spans[0])
        clear(hb2_ref, n_in - 2, *spans[1])

        lo0, hi0 = spans[0]
        mask0 = mask_ref[0, :, lo0:hi0] > 0.5
        group = 8
        filler = jnp.zeros((group, hi0 - lo0), jnp.float32)
        for g in range(vp_ref.shape[0] // group):
            v = vp_ref[g * group:(g + 1) * group, :]
            rows = [pltpu.roll(v, sh, 1)[:, lo0:hi0] if sh else v[:, lo0:hi0] for sh in shifts]
            patch = jnp.concatenate(rows + [filler], axis=0).astype(jnp.bfloat16)
            patch = jnp.concatenate([patch, patch], axis=0)
            acc = jnp.dot(wst_ref[...], patch, preferred_element_type=jnp.float32)
            for j in range(group):
                f = g * group + j
                if f >= n_in:
                    break
                part = acc[j * channels:(j + 1) * channels]
                h0 = jnp.maximum(part + bst_ref[...], 0.0).astype(jnp.bfloat16)
                keep = mask0 & (first + f >= 0)
                ha_ref[f, :, base + lo0:base + hi0] = jnp.where(keep, h0, jnp.zeros_like(h0))

        def spatial(block, src_ref, n, wide, lo, hi):
            lo_y, hi_y = wide
            width_y = hi_y - lo_y
            dx_shifts = [(-(base + dx - 1)) % total for dx in range(3)]
            a, b = lo - lo_y, hi - lo_y
            rows = 3 * channels
            for g0 in range(0, n, SPATIAL_GROUP):
                frames = [min(g0 + j, n - 1) for j in range(SPATIAL_GROUP)]
                pieces = []
                for f in frames:
                    x = src_ref[f]
                    pieces += [pltpu.roll(x, sh, 1)[:, lo_y:hi_y] for sh in dx_shifts]
                patches = jnp.concatenate(pieces, axis=0)
                y = jnp.dot(wsp_ref[block], patches, preferred_element_type=jnp.float32)
                for j in range(min(SPATIAL_GROUP, n - g0)):
                    part = y[j * rows:(j + 1) * rows]
                    up = pltpu.roll(part[0:channels], pitch, 1)[:, a:b]
                    down = pltpu.roll(part[2 * channels:3 * channels], width_y - pitch, 1)[:, a:b]
                    acc = up + part[channels:2 * channels, a:b] + down
                    s_ref[g0 + j, :, lo:hi] = acc.astype(jnp.bfloat16)

        def temporal(block, src_ref, n_out, lo, hi, finish):
            for k0 in range(0, n_out, group):
                stacked = jnp.concatenate([s_ref[k0 + jj, :, lo:hi] for jj in range(group + 2)], axis=0)
                acc = jnp.dot(tw_ref[block], stacked, preferred_element_type=jnp.float32)
                for j in range(min(group, n_out - k0)):
                    k = k0 + j
                    part = acc[j * channels:(j + 1) * channels] + tb_ref[block]
                    centre = src_ref[k + 2, :, base + lo:base + hi].astype(jnp.float32)
                    finish(k, (centre + jnp.maximum(part, 0.0)).astype(jnp.bfloat16))

        s_ref[n_in:, :, :] = jnp.zeros((s_ref.shape[0] - n_in, channels, length), jnp.bfloat16)
        lo1, hi1 = spans[1]
        spatial(0, ha_ref, n_in, spans[0], lo1, hi1)
        mask1 = mask_ref[1, :, lo1:hi1] > 0.5

        def finish0(k, h1):
            keep = mask1 & (first + 2 + k >= 0)
            hb2_ref[k, :, base + lo1:base + hi1] = jnp.where(keep, h1, jnp.zeros_like(h1))

        temporal(0, ha_ref, n_in - 2, lo1, hi1, finish0)
        lo2, hi2 = spans[2]
        spatial(1, hb2_ref, n_in - 2, spans[1], lo2, hi2)

        def finish1(k, h2):
            head = jnp.sum(hw_ref[...] * h2.astype(jnp.float32), axis=0, keepdims=True) + hb_ref[...]
            out_ref[k:k + 1, lo2:hi2] = head

        temporal(1, hb2_ref, count, lo2, hi2, finish1)

    return kernel


def shards(video, stem_weight, stem_bias, spatial_weight, temporal_weight, temporal_bias, head_weight, head_bias):
    clip = video[:, 0]
    count, height, width = clip.shape
    lead = shifted(clip[-LEAD:], "tm", 1)
    extended = spread(jnp.concatenate([lead, clip], axis=0), HALO)
    n_in = count + LEAD
    pitch = width + 2 * HALO
    rows = height + 2 * HALO
    length = round_up(rows * pitch, 128)
    base = round_up(pitch + 1, 128)
    total = length + 2 * base
    flat = extended.reshape(n_in, rows * pitch)
    n_pad = round_up(n_in, 8)
    flat = jnp.pad(flat.astype(jnp.float32), ((0, n_pad - n_in), (base, total - base - rows * pitch)))
    vp = flat

    channels = stem_weight.shape[1]
    w_hi = stem_weight.astype(jnp.bfloat16).astype(jnp.float32)
    w_lo = stem_weight - w_hi
    eye = jnp.eye(8, dtype=jnp.float32)

    def spread_taps(w):
        w = jnp.pad(w, ((0, 1), (0, 0)))
        return jnp.einsum("to,jk->jotk", w, eye).reshape(8 * channels, 8 * w.shape[0])

    wst = jnp.concatenate([spread_taps(w_hi), spread_taps(w_lo)], axis=1).astype(jnp.bfloat16)
    bst = stem_bias.astype(jnp.float32)[:, None]
    wsp = spatial_weight.reshape(2, 3, 3, channels, channels).transpose(0, 1, 3, 2, 4)
    wsp = wsp.reshape(2, 3 * channels, 3 * channels)
    wsp = jnp.einsum("jk,bmn->bjmkn", jnp.eye(SPATIAL_GROUP, dtype=jnp.float32), wsp.astype(jnp.float32))
    wsp = wsp.reshape(2, SPATIAL_GROUP * 3 * channels, SPATIAL_GROUP * 3 * channels).astype(jnp.bfloat16)
    band = jnp.stack([jnp.eye(8, 10, d, dtype=jnp.float32) for d in range(3)])
    tw = jnp.einsum("dja,bdoi->bjoai", band, temporal_weight.astype(jnp.float32))
    tw = tw.reshape(2, 8 * channels, 10 * channels).astype(jnp.bfloat16)
    tb = temporal_bias.astype(jnp.float32)[:, :, None]
    hw = head_weight.astype(jnp.float32)[:, None]
    hb = head_bias.astype(jnp.float32).reshape(1, 1)
    masks = flat_masks(height, width, length)
    first = (lax.axis_index("tm") * count - LEAD).astype(jnp.int32).reshape(1)

    vmem = pltpu.MemorySpace.VMEM if hasattr(pltpu, "MemorySpace") else pltpu.TPUMemorySpace.VMEM
    smem = pltpu.MemorySpace.SMEM if hasattr(pltpu, "MemorySpace") else pltpu.TPUMemorySpace.SMEM
    spec = pl.BlockSpec(memory_space=vmem)
    out = pl.pallas_call(
        make_kernel(n_in, count, pitch, length, base, total, height),
        out_shape=jax.ShapeDtypeStruct((count, length), jnp.float32),
        in_specs=[pl.BlockSpec(memory_space=smem)] + [spec] * 9,
        out_specs=spec,
        scratch_shapes=[
            pltpu.VMEM((n_in, channels, total), jnp.bfloat16),
            pltpu.VMEM((n_in - 2, channels, total), jnp.bfloat16),
            pltpu.VMEM((round_up(n_in - 2, 8) + 2, channels, length), jnp.bfloat16),
        ],
        compiler_params=pltpu.CompilerParams(vmem_limit_bytes=48 * 1024 * 1024),
    )(first, vp, masks, wst, bst, wsp, tw, tb, hw, hb)
    result = out[:, : rows * pitch].reshape(count, rows, pitch)
    result = result[:, HALO:HALO + height, HALO:HALO + width]
    return result[:, None]


def solution(mesh):
    placed = (P("tm", "space", None, None), P(), P(), P(), P(), P(), P(), P())
    return jax.shard_map(
        shards, mesh=mesh, in_specs=placed, out_specs=P("tm", "space", None, None), check_vma=False
    )
```

```python
import jax
import jax.numpy as jnp
from jax import lax
from jax.experimental import pallas as pl
from jax.experimental.pallas import tpu as pltpu
from jax.sharding import PartitionSpec as P

HALO = 3
LEAD = 4
SPATIAL_GROUP = 4


def shifted(value, axis, steps):
    count = lax.axis_size(axis)
    leading, last = (max(0, -steps), min(count, count - steps))
    if leading >= last:
        return jnp.zeros_like(value)
    return lax.ppermute(value, axis, [(source, source + steps) for source in range(leading, last)])


def grid_shape():
    parts = lax.axis_size("space")
    grid_w = min(4, parts)
    return parts // grid_w, grid_w


def spread(field, width):
    grid_w = grid_shape()[1]
    column = lax.axis_index("space") % grid_w
    west_piece = field[..., -width:]
    east_piece = field[..., :width]
    west_piece = jnp.where(column < grid_w - 1, west_piece, jnp.zeros_like(west_piece))
    east_piece = jnp.where(column > 0, east_piece, jnp.zeros_like(east_piece))
    west = shifted(west_piece, "space", 1)
    east = shifted(east_piece, "space", -1)
    wide = jnp.concatenate([west, field, east], axis=-1)
    north = shifted(wide[..., -width:, :], "space", grid_w)
    south = shifted(wide[..., :width, :], "space", -grid_w)
    return jnp.concatenate([north, wide, south], axis=-2)


def round_up(value, step):
    return (value + step - 1) // step * step


def flat_masks(height, width, length):
    grid_h, grid_w = grid_shape()
    place = lax.axis_index("space")
    pitch = width + 2 * HALO
    q = jnp.arange(length)
    y = q // pitch - HALO
    x = q % pitch - HALO
    gy = place // grid_w * height + y
    gx = place % grid_w * width + x
    inside = (q < (height + 2 * HALO) * pitch) & (gy >= 0) & (gy < grid_h * height)
    inside = inside & (gx >= 0) & (gx < grid_w * width)
    rows = []
    for margin in (2, 1):
        keep = inside & (y >= -margin) & (y < height + margin) & (x >= -margin) & (x < width + margin)
        rows.append(keep.astype(jnp.float32))
    return jnp.stack(rows)[:, None, :]


def make_kernel(n_in, count, pitch, length, base, total, height):
    offs = [(dy - 1) * pitch + (dx - 1) for dy in range(3) for dx in range(3)]
    shifts = [(-(base + off)) % total for off in offs]

    def span(margin):
        lo = (HALO - margin) * pitch // 128 * 128
        hi = min(length, round_up((HALO + height + margin) * pitch, 128))
        return lo, hi

    spans = [span(2), span(1), span(0)]

    def kernel(first_ref, vp_ref, mask_ref, wst_ref, bst_ref, wsp_ref, tw_ref, tb_ref, hw_ref, hb_ref,
               out_ref, ha_ref, hb2_ref, s_ref):
        first = first_ref[0]
        channels = ha_ref.shape[1]

        def clear(ref, n, lo, hi):
            front = jnp.zeros((channels, base + lo), jnp.bfloat16)
            back = jnp.zeros((channels, total - base - hi), jnp.bfloat16)

            def body(f, carry):
                ref[f, :, 0:base + lo] = front
                ref[f, :, base + hi:total] = back
                return carry
            lax.fori_loop(0, n, body, 0)

        clear(ha_ref, n_in, *spans[0])
        clear(hb2_ref, n_in - 2, *spans[1])

        lo0, hi0 = spans[0]
        mask0 = mask_ref[0, :, lo0:hi0] > 0.5
        group = 8
        filler = jnp.zeros((group, hi0 - lo0), jnp.float32)
        for g in range(vp_ref.shape[0] // group):
            v = vp_ref[g * group:(g + 1) * group, :]
            rows = [pltpu.roll(v, sh, 1)[:, lo0:hi0] if sh else v[:, lo0:hi0] for sh in shifts]
            patch = jnp.concatenate(rows + [filler], axis=0).astype(jnp.bfloat16)
            patch = jnp.concatenate([patch, patch], axis=0)
            acc = jnp.dot(wst_ref[...], patch, preferred_element_type=jnp.float32)
            for j in range(group):
                f = g * group + j
                if f >= n_in:
                    break
                part = acc[j * channels:(j + 1) * channels]
                h0 = jnp.maximum(part + bst_ref[...], 0.0).astype(jnp.bfloat16)
                keep = mask0 & (first + f >= 0)
                ha_ref[f, :, base + lo0:base + hi0] = jnp.where(keep, h0, jnp.zeros_like(h0))

        def spatial(block, src_ref, n, wide, lo, hi):
            lo_y, hi_y = wide
            width_y = hi_y - lo_y
            dx_shifts = [(-(base + dx - 1)) % total for dx in range(3)]
            a, b = lo - lo_y, hi - lo_y
            rows = 3 * channels
            for g0 in range(0, n, SPATIAL_GROUP):
                frames = [min(g0 + j, n - 1) for j in range(SPATIAL_GROUP)]
                pieces = []
                for f in frames:
                    x = src_ref[f]
                    pieces += [pltpu.roll(x, sh, 1)[:, lo_y:hi_y] for sh in dx_shifts]
                patches = jnp.concatenate(pieces, axis=0)
                y = jnp.dot(wsp_ref[block], patches, preferred_element_type=jnp.float32)
                for j in range(min(SPATIAL_GROUP, n - g0)):
                    part = y[j * rows:(j + 1) * rows]
                    up = pltpu.roll(part[0:channels], pitch, 1)[:, a:b]
                    down = pltpu.roll(part[2 * channels:3 * channels], width_y - pitch, 1)[:, a:b]
                    acc = up + part[channels:2 * channels, a:b] + down
                    s_ref[g0 + j, :, lo:hi] = acc.astype(jnp.bfloat16)

        def temporal(block, src_ref, n_out, lo, hi, finish):
            for k0 in range(0, n_out, group):
                stacked = jnp.concatenate([s_ref[k0 + jj, :, lo:hi] for jj in range(group + 2)], axis=0)
                acc = jnp.dot(tw_ref[block], stacked, preferred_element_type=jnp.float32)
                done = []
                for j in range(min(group, n_out - k0)):
                    k = k0 + j
                    part = acc[j * channels:(j + 1) * channels] + tb_ref[block]
                    centre = src_ref[k + 2, :, base + lo:base + hi].astype(jnp.float32)
                    done.append(finish(k, (centre + jnp.maximum(part, 0.0)).astype(jnp.bfloat16)))
                if done[0] is not None:
                    done += [jnp.zeros_like(done[0])] * (group - len(done))
                    stacked_h = jnp.concatenate(done, axis=0)
                    heads = jnp.dot(hw_ref[...], jnp.concatenate([stacked_h, stacked_h], axis=0),
                                    preferred_element_type=jnp.float32) + hb_ref[...]
                    out_ref[k0:k0 + group, lo:hi] = heads

        s_ref[n_in:, :, :] = jnp.zeros((s_ref.shape[0] - n_in, channels, length), jnp.bfloat16)
        lo1, hi1 = spans[1]
        spatial(0, ha_ref, n_in, spans[0], lo1, hi1)
        mask1 = mask_ref[1, :, lo1:hi1] > 0.5

        def finish0(k, h1):
            keep = mask1 & (first + 2 + k >= 0)
            hb2_ref[k, :, base + lo1:base + hi1] = jnp.where(keep, h1, jnp.zeros_like(h1))

        temporal(0, ha_ref, n_in - 2, lo1, hi1, finish0)
        lo2, hi2 = spans[2]
        spatial(1, hb2_ref, n_in - 2, spans[1], lo2, hi2)

        def finish1(k, h2):
            return h2

        temporal(1, hb2_ref, count, lo2, hi2, finish1)

    return kernel


def shards(video, stem_weight, stem_bias, spatial_weight, temporal_weight, temporal_bias, head_weight, head_bias):
    clip = video[:, 0]
    count, height, width = clip.shape
    lead = shifted(clip[-LEAD:], "tm", 1)
    extended = spread(jnp.concatenate([lead, clip], axis=0), HALO)
    n_in = count + LEAD
    pitch = width + 2 * HALO
    rows = height + 2 * HALO
    length = round_up(rows * pitch, 128)
    base = round_up(pitch + 1, 128)
    total = length + 2 * base
    flat = extended.reshape(n_in, rows * pitch)
    n_pad = round_up(n_in, 8)
    flat = jnp.pad(flat.astype(jnp.float32), ((0, n_pad - n_in), (base, total - base - rows * pitch)))
    vp = flat

    channels = stem_weight.shape[1]
    w_hi = stem_weight.astype(jnp.bfloat16).astype(jnp.float32)
    w_lo = stem_weight - w_hi
    eye = jnp.eye(8, dtype=jnp.float32)

    def spread_taps(w):
        w = jnp.pad(w, ((0, 1), (0, 0)))
        return jnp.einsum("to,jk->jotk", w, eye).reshape(8 * channels, 8 * w.shape[0])

    wst = jnp.concatenate([spread_taps(w_hi), spread_taps(w_lo)], axis=1).astype(jnp.bfloat16)
    bst = stem_bias.astype(jnp.float32)[:, None]
    wsp = spatial_weight.reshape(2, 3, 3, channels, channels).transpose(0, 1, 3, 2, 4)
    wsp = wsp.reshape(2, 3 * channels, 3 * channels)
    wsp = jnp.einsum("jk,bmn->bjmkn", jnp.eye(SPATIAL_GROUP, dtype=jnp.float32), wsp.astype(jnp.float32))
    wsp = wsp.reshape(2, SPATIAL_GROUP * 3 * channels, SPATIAL_GROUP * 3 * channels).astype(jnp.bfloat16)
    band = jnp.stack([jnp.eye(8, 10, d, dtype=jnp.float32) for d in range(3)])
    tw = jnp.einsum("dja,bdoi->bjoai", band, temporal_weight.astype(jnp.float32))
    tw = tw.reshape(2, 8 * channels, 10 * channels).astype(jnp.bfloat16)
    tb = temporal_bias.astype(jnp.float32)[:, :, None]
    hw_hi = head_weight.astype(jnp.bfloat16).astype(jnp.float32)
    hw_lo = head_weight - hw_hi
    frame_eye = jnp.eye(8, dtype=jnp.float32)
    hw = jnp.concatenate([jnp.einsum("jk,c->jkc", frame_eye, w).reshape(8, 8 * channels) for w in (hw_hi, hw_lo)], axis=1)
    hw = hw.astype(jnp.bfloat16)
    hb = head_bias.astype(jnp.float32).reshape(1, 1)
    masks = flat_masks(height, width, length)
    first = (lax.axis_index("tm") * count - LEAD).astype(jnp.int32).reshape(1)

    vmem = pltpu.MemorySpace.VMEM if hasattr(pltpu, "MemorySpace") else pltpu.TPUMemorySpace.VMEM
    smem = pltpu.MemorySpace.SMEM if hasattr(pltpu, "MemorySpace") else pltpu.TPUMemorySpace.SMEM
    spec = pl.BlockSpec(memory_space=vmem)
    out = pl.pallas_call(
        make_kernel(n_in, count, pitch, length, base, total, height),
        out_shape=jax.ShapeDtypeStruct((round_up(count, 8), length), jnp.float32),
        in_specs=[pl.BlockSpec(memory_space=smem)] + [spec] * 9,
        out_specs=spec,
        scratch_shapes=[
            pltpu.VMEM((n_in, channels, total), jnp.bfloat16),
            pltpu.VMEM((n_in - 2, channels, total), jnp.bfloat16),
            pltpu.VMEM((round_up(n_in - 2, 8) + 2, channels, length), jnp.bfloat16),
        ],
        compiler_params=pltpu.CompilerParams(vmem_limit_bytes=48 * 1024 * 1024),
    )(first, vp, masks, wst, bst, wsp, tw, tb, hw, hb)
    result = out[:count, : rows * pitch].reshape(count, rows, pitch)
    result = result[:, HALO:HALO + height, HALO:HALO + width]
    return result[:, None]


def solution(mesh):
    placed = (P("tm", "space", None, None), P(), P(), P(), P(), P(), P(), P())
    return jax.shard_map(
        shards, mesh=mesh, in_specs=placed, out_specs=P("tm", "space", None, None), check_vma=False
    )
```

```python
import jax
import jax.numpy as jnp
from jax import lax
from jax.experimental import pallas as pl
from jax.experimental.pallas import tpu as pltpu
from jax.sharding import PartitionSpec as P

HALO = 3
LEAD = 4
SPATIAL_GROUP = 4


def shifted(value, axis, steps):
    count = lax.axis_size(axis)
    leading, last = (max(0, -steps), min(count, count - steps))
    if leading >= last:
        return jnp.zeros_like(value)
    return lax.ppermute(value, axis, [(source, source + steps) for source in range(leading, last)])


def grid_shape():
    parts = lax.axis_size("space")
    grid_w = min(4, parts)
    return parts // grid_w, grid_w


def spread(field, width):
    grid_w = grid_shape()[1]
    column = lax.axis_index("space") % grid_w
    west_piece = field[..., -width:]
    east_piece = field[..., :width]
    west_piece = jnp.where(column < grid_w - 1, west_piece, jnp.zeros_like(west_piece))
    east_piece = jnp.where(column > 0, east_piece, jnp.zeros_like(east_piece))
    west = shifted(west_piece, "space", 1)
    east = shifted(east_piece, "space", -1)
    wide = jnp.concatenate([west, field, east], axis=-1)
    north = shifted(wide[..., -width:, :], "space", grid_w)
    south = shifted(wide[..., :width, :], "space", -grid_w)
    return jnp.concatenate([north, wide, south], axis=-2)


def round_up(value, step):
    return (value + step - 1) // step * step


def flat_masks(height, width, length):
    grid_h, grid_w = grid_shape()
    place = lax.axis_index("space")
    pitch = width + 2 * HALO
    q = jnp.arange(length)
    y = q // pitch - HALO
    x = q % pitch - HALO
    gy = place // grid_w * height + y
    gx = place % grid_w * width + x
    inside = (q < (height + 2 * HALO) * pitch) & (gy >= 0) & (gy < grid_h * height)
    inside = inside & (gx >= 0) & (gx < grid_w * width)
    rows = []
    for margin in (2, 1):
        keep = inside & (y >= -margin) & (y < height + margin) & (x >= -margin) & (x < width + margin)
        rows.append(keep.astype(jnp.float32))
    return jnp.stack(rows)[:, None, :]


def make_kernel(n_in, count, pitch, length, base, total, height):
    offs = [(dy - 1) * pitch + (dx - 1) for dy in range(3) for dx in range(3)]
    shifts = [(-(base + off)) % total for off in offs]

    def span(margin):
        lo = (HALO - margin) * pitch // 128 * 128
        hi = min(length, round_up((HALO + height + margin) * pitch, 128))
        return lo, hi

    spans = [span(2), span(1), span(0)]

    def kernel(first_ref, vp_ref, mask_ref, wst_ref, bst_ref, wsp_ref, tw_ref, tb_ref, hw_ref, hb_ref,
               out_ref, ha_ref, hb2_ref, s_ref):
        first = first_ref[0]
        channels = ha_ref.shape[1]

        def clear(ref, n, lo, hi):
            front = jnp.zeros((channels, base + lo), jnp.bfloat16)
            back = jnp.zeros((channels, total - base - hi), jnp.bfloat16)

            def body(f, carry):
                ref[f, :, 0:base + lo] = front
                ref[f, :, base + hi:total] = back
                return carry
            lax.fori_loop(0, n, body, 0)

        clear(ha_ref, n_in, *spans[0])
        clear(hb2_ref, n_in - 2, *spans[1])

        lo0, hi0 = spans[0]
        mask0 = mask_ref[0, :, lo0:hi0] > 0.5
        group = 8
        filler = jnp.zeros((group, hi0 - lo0), jnp.float32)
        for g in range(vp_ref.shape[0] // group):
            v = vp_ref[g * group:(g + 1) * group, :]
            rows = [pltpu.roll(v, sh, 1)[:, lo0:hi0] if sh else v[:, lo0:hi0] for sh in shifts]
            patch = jnp.concatenate(rows + [filler], axis=0).astype(jnp.bfloat16)
            patch = jnp.concatenate([patch, patch], axis=0)
            acc = jnp.dot(wst_ref[...], patch, preferred_element_type=jnp.float32)
            for j in range(group):
                f = g * group + j
                if f >= n_in:
                    break
                part = acc[j * channels:(j + 1) * channels]
                h0 = jnp.maximum(part + bst_ref[...], 0.0).astype(jnp.bfloat16)
                keep = mask0 & (first + f >= 0)
                ha_ref[f, :, base + lo0:base + hi0] = jnp.where(keep, h0, jnp.zeros_like(h0))

        def spatial(block, src_ref, n, wide, lo, hi):
            lo_y, hi_y = wide
            width_y = hi_y - lo_y
            dx_shifts = [(-(base + dx - 1)) % total for dx in range(3)]
            a, b = lo - lo_y, hi - lo_y
            rows = 3 * channels
            for g0 in range(0, n, SPATIAL_GROUP):
                frames = [min(g0 + j, n - 1) for j in range(SPATIAL_GROUP)]
                pieces = []
                for f in frames:
                    x = src_ref[f]
                    pieces += [pltpu.roll(x, sh, 1)[:, lo_y:hi_y] for sh in dx_shifts]
                patches = jnp.concatenate(pieces, axis=0)
                y = jnp.dot(wsp_ref[block], patches, preferred_element_type=jnp.float32)
                for j in range(min(SPATIAL_GROUP, n - g0)):
                    part = y[j * rows:(j + 1) * rows]
                    up = pltpu.roll(part[0:channels], pitch, 1)[:, a:b]
                    down = pltpu.roll(part[2 * channels:3 * channels], width_y - pitch, 1)[:, a:b]
                    acc = up + part[channels:2 * channels, a:b] + down
                    s_ref[g0 + j, :, lo:hi] = acc.astype(jnp.bfloat16)

        def temporal(block, src_ref, n_out, lo, hi, finish):
            for k0 in range(0, n_out, group):
                stacked = jnp.concatenate([s_ref[k0 + jj, :, lo:hi] for jj in range(group + 2)], axis=0)
                acc = jnp.dot(tw_ref[block], stacked, preferred_element_type=jnp.float32)
                done = []
                for j in range(min(group, n_out - k0)):
                    k = k0 + j
                    part = acc[j * channels:(j + 1) * channels] + tb_ref[block]
                    centre = src_ref[k + 2, :, base + lo:base + hi].astype(jnp.float32)
                    done.append(finish(k, (centre + jnp.maximum(part, 0.0)).astype(jnp.bfloat16)))
                if done[0] is not None:
                    done += [jnp.zeros_like(done[0])] * (group - len(done))
                    stacked_h = jnp.concatenate(done, axis=0)
                    heads = jnp.dot(hw_ref[...], jnp.concatenate([stacked_h, stacked_h], axis=0),
                                    preferred_element_type=jnp.float32) + hb_ref[...]
                    out_ref[k0:k0 + group, lo:hi] = heads

        s_ref[n_in:, :, :] = jnp.zeros((s_ref.shape[0] - n_in, channels, length), jnp.bfloat16)
        lo1, hi1 = spans[1]
        spatial(0, ha_ref, n_in, spans[0], lo1, hi1)
        mask1 = mask_ref[1, :, lo1:hi1] > 0.5

        def finish0(k, h1):
            keep = mask1 & (first + 2 + k >= 0)
            hb2_ref[k, :, base + lo1:base + hi1] = jnp.where(keep, h1, jnp.zeros_like(h1))

        temporal(0, ha_ref, n_in - 2, lo1, hi1, finish0)
        lo2, hi2 = spans[2]
        spatial(1, hb2_ref, n_in - 2, spans[1], lo2, hi2)

        def finish1(k, h2):
            return h2

        temporal(1, hb2_ref, count, lo2, hi2, finish1)

    return kernel


def shards(video, stem_weight, stem_bias, spatial_weight, temporal_weight, temporal_bias, head_weight, head_bias):
    clip = video[:, 0]
    count, height, width = clip.shape
    lead = shifted(clip[-LEAD:], "tm", 1)
    extended = spread(jnp.concatenate([lead, clip], axis=0), HALO)
    n_in = count + LEAD
    pitch = width + 2 * HALO
    rows = height + 2 * HALO
    length = round_up(rows * pitch, 128)
    base = round_up(pitch + 1, 128)
    total = length + 2 * base
    flat = extended.reshape(n_in, rows * pitch)
    n_pad = round_up(n_in, 8)
    flat = jnp.pad(flat.astype(jnp.float32), ((0, n_pad - n_in), (base, total - base - rows * pitch)))
    vp = flat

    channels = stem_weight.shape[1]
    w_hi = lax.reduce_precision(stem_weight, exponent_bits=8, mantissa_bits=7)
    w_lo = stem_weight - w_hi
    eye = jnp.eye(8, dtype=jnp.float32)

    def spread_taps(w):
        w = jnp.pad(w, ((0, 1), (0, 0)))
        return jnp.einsum("to,jk->jotk", w, eye).reshape(8 * channels, 8 * w.shape[0])

    wst = jnp.concatenate([spread_taps(w_hi), spread_taps(w_lo)], axis=1).astype(jnp.bfloat16)
    bst = stem_bias.astype(jnp.float32)[:, None]
    wsp = spatial_weight.reshape(2, 3, 3, channels, channels).transpose(0, 1, 3, 2, 4)
    wsp = wsp.reshape(2, 3 * channels, 3 * channels)
    wsp = jnp.einsum("jk,bmn->bjmkn", jnp.eye(SPATIAL_GROUP, dtype=jnp.float32), wsp.astype(jnp.float32))
    wsp = wsp.reshape(2, SPATIAL_GROUP * 3 * channels, SPATIAL_GROUP * 3 * channels).astype(jnp.bfloat16)
    band = jnp.stack([jnp.eye(8, 10, d, dtype=jnp.float32) for d in range(3)])
    tw = jnp.einsum("dja,bdoi->bjoai", band, temporal_weight.astype(jnp.float32))
    tw = tw.reshape(2, 8 * channels, 10 * channels).astype(jnp.bfloat16)
    tb = temporal_bias.astype(jnp.float32)[:, :, None]
    hw_hi = lax.reduce_precision(head_weight.astype(jnp.float32), exponent_bits=8, mantissa_bits=7)
    hw_lo = head_weight - hw_hi
    frame_eye = jnp.eye(8, dtype=jnp.float32)
    hw = jnp.concatenate([jnp.einsum("jk,c->jkc", frame_eye, w).reshape(8, 8 * channels) for w in (hw_hi, hw_lo)], axis=1)
    hw = hw.astype(jnp.bfloat16)
    hb = head_bias.astype(jnp.float32).reshape(1, 1)
    masks = flat_masks(height, width, length)
    first = (lax.axis_index("tm") * count - LEAD).astype(jnp.int32).reshape(1)

    vmem = pltpu.MemorySpace.VMEM if hasattr(pltpu, "MemorySpace") else pltpu.TPUMemorySpace.VMEM
    smem = pltpu.MemorySpace.SMEM if hasattr(pltpu, "MemorySpace") else pltpu.TPUMemorySpace.SMEM
    spec = pl.BlockSpec(memory_space=vmem)
    out = pl.pallas_call(
        make_kernel(n_in, count, pitch, length, base, total, height),
        out_shape=jax.ShapeDtypeStruct((round_up(count, 8), length), jnp.float32),
        in_specs=[pl.BlockSpec(memory_space=smem)] + [spec] * 9,
        out_specs=spec,
        scratch_shapes=[
            pltpu.VMEM((n_in, channels, total), jnp.bfloat16),
            pltpu.VMEM((n_in - 2, channels, total), jnp.bfloat16),
            pltpu.VMEM((round_up(n_in - 2, 8) + 2, channels, length), jnp.bfloat16),
        ],
        compiler_params=pltpu.CompilerParams(vmem_limit_bytes=48 * 1024 * 1024),
    )(first, vp, masks, wst, bst, wsp, tw, tb, hw, hb)
    result = out[:count, : rows * pitch].reshape(count, rows, pitch)
    result = result[:, HALO:HALO + height, HALO:HALO + width]
    return result[:, None]


def solution(mesh):
    placed = (P("tm", "space", None, None), P(), P(), P(), P(), P(), P(), P())
    return jax.shard_map(
        shards, mesh=mesh, in_specs=placed, out_specs=P("tm", "space", None, None), check_vma=False
    )
```
